128 devices in a mesh: tm: 2 (over core), space: 64 (over z, y, x).
Axes of the slice: x: 4, y: 4, z: 4, core: 2. Of those that a mesh axis runs over, the one named last changes fastest.
Arguments:
- increment_start: float32 [2, 8, 2048, 1024], P('tm', None, 'space'), may hold values from -6 to 6
- dual_model_start: float32 [2, 8, 2048, 1024], P('tm', None, 'space'), may hold values from -6 to 6
- dual_obs_start: bfloat16 [2, 1024, 128], P('tm', 'space'), may hold values from -6 to 6
- model_rhs: float32 [2, 8, 2048, 1024], P('tm', None, 'space'), may hold values from -6 to 6
- err_var: float32 [2, 8, 2048, 1024], P('tm', None, 'space'), may hold values from 0.2 to 2
- decays: float32 [2, 8, 2048, 1024], P('tm', None, 'space'), may hold values from 0.1 to 0.95
- scaling: float32 [8, 2048, 1024], P(None, 'space'), may hold values from 0.5 to 1
- diffusion: float32 [8], replicated, may hold values from 0.05 to 0.24
- owners: int32 [2, 1024], P('tm', 'space'), may hold values from 0 to 63, as said below
- tile_cols: int32 [2, 1024, 128], P('tm', 'space'), may hold values from 0 to 32767, as said below
- jacobian: bfloat16 [2, 1024, 128, 1024], P('tm', 'space'), may hold values from -0.1875 to 0.1875
- innovation: bfloat16 [2, 1024, 128], P('tm', 'space'), may hold values from -6 to 6
- obs_var: bfloat16 [2, 1024, 128], P('tm', 'space'), may hold values from 0.5 to 4
Outputs:
- dual_model: float32 [2, 8, 2048, 1024], P('tm', None, 'space')
- dual_obs: float32 [2, 1024, 128], P('tm', 'space')
- increment: float32 [2, 8, 2048, 1024], P('tm', None, 'space')
The draws below stay inside these ranges and needn't reach their ends.
Inputs may be any that keep to these rules, and one draw needn't show every extreme that they name: `owners`: in each subwindow at most 2 of the 16 tiles of one device name the same owner, and one owner is named exactly 2 times by the tiles of every device. All 128 cells of a tile lie in one latitude row: tile_cols[k, t, c] // 1024 is the same for every c.
All inputs are finite; a program needn't handle non-finite values.
Results may differ from the reference program's by a relative error of at most 0.0042.
The reference program's roundings to bfloat16 on the way (of `gathered` and `tile_grad`) count: a program that leaves them out, or rounds other values in their place, can miss the bound.
Values may be sent and summed in bfloat16 or wider, within the bound.
No kernel may reach another device: no remote copies, remote signals or barrier semaphores. Data moves between devices by JAX's collectives and lax.ppermute only.
A program may use at most 256 MiB of HBM per device.

```python
import math
import jax
import jax.numpy as jnp
from jax import lax

LEV = 8
TY = 32
LON = 1024
OBT_DEV = 16
OROWS = 128
TCOLS = 128
SUBSTEPS = 2
ITERS = 2
SUBWIN = 2
NY = 2048
TILES = 1024
CAP = 2
N_TM = 2
N_SPACE = 64


def draw_owners(key, part):
    pool_size = (N_SPACE - 1) * CAP
    hot_owner = jax.random.randint(jax.random.fold_in(key, 11), (N_TM, 1, 1), 0, N_SPACE)
    base_owner = jnp.arange(pool_size, dtype=jnp.int32) // CAP
    others = base_owner[None, None, :] + (base_owner[None, None, :] >= hot_owner).astype(jnp.int32)
    others = jnp.broadcast_to(others, (N_TM, N_SPACE, pool_size))
    scores = jax.random.randint(jax.random.fold_in(key, 12), (N_TM, N_SPACE, pool_size), 0, 2 ** 20) * pool_size
    scores = scores + jnp.arange(pool_size, dtype=jnp.int32)[None, None, :]
    order = jnp.argsort(scores, axis=-1)
    picked = jnp.take_along_axis(others, order, axis=-1)[:, :, :OBT_DEV - CAP]
    hot_rows = jnp.broadcast_to(hot_owner, (N_TM, N_SPACE, CAP))
    tiles_all = jnp.concatenate([hot_rows, picked], axis=-1)
    shuffle = jax.random.randint(jax.random.fold_in(key, 13), (N_TM, N_SPACE, OBT_DEV), 0, 2 ** 20) * OBT_DEV
    shuffle = shuffle + jnp.arange(OBT_DEV, dtype=jnp.int32)[None, None, :]
    placed = jnp.take_along_axis(tiles_all, jnp.argsort(shuffle, axis=-1), axis=-1)
    return placed.reshape(N_TM, N_SPACE * OBT_DEV).astype(jnp.int32)


def draw_tile_cols(key, part):
    row_pick = jax.random.randint(jax.random.fold_in(key, 21), (SUBWIN, TILES, 1), 0, TY)
    col_pick = jax.random.randint(jax.random.fold_in(key, 22), (SUBWIN, TILES, TCOLS), 0, LON)
    return (row_pick * LON + col_pick).astype(jnp.int32)


def shard_levels(key, dims, split, smallest, top_value):
    def one(position, shards_of):
        steps = jax.random.uniform(jax.random.fold_in(jax.random.fold_in(key, 6), position), (shards_of,), jnp.float32, smallest / len(split), top_value / len(split))
        return jnp.repeat(jnp.exp(steps), dims[position] // shards_of).reshape((-1,) + (1,) * (len(dims) - position - 1))

    loudness = one(*split[0])
    for cut in split[1:]:
        loudness = loudness * one(*cut)
    return loudness


def scatter_about(own_key, shape, deviation, most, pieces=(), kind=jnp.bfloat16):
    values = deviation * jax.random.normal(own_key, shape, jnp.float32)
    if pieces:
        values = values * shard_levels(own_key, shape, pieces, -0.22, 0.18)
    return jnp.clip(values, -most, most).astype(kind)


def setup_inputs(seed: int = 0) -> dict:
    keys = jax.random.split(jax.random.key(seed), 14)
    return {
        "increment_start": scatter_about(keys[0], (SUBWIN, LEV, NY, LON), 1.0, 6.0, ((0, 2), (2, 64)), jnp.float32),
        "dual_model_start": scatter_about(keys[1], (SUBWIN, LEV, NY, LON), 0.5, 6.0, ((0, 2), (2, 64)), jnp.float32),
        "dual_obs_start": scatter_about(keys[2], (SUBWIN, TILES, OROWS), 0.5, 6.0, ((0, 2), (1, 64))),
        "model_rhs": scatter_about(keys[3], (SUBWIN, LEV, NY, LON), 1.0, 6.0, ((0, 2), (2, 64)), jnp.float32),
        "err_var": jnp.clip(jnp.exp(math.log(2.0) - 2.3025851 * jax.random.uniform(keys[4], (SUBWIN, LEV, NY, LON), jnp.float32) ** shard_levels(keys[4], (SUBWIN, LEV, NY, LON), ((0, 2), (2, 64)), -0.2, 0.2)), 0.2, 2.0),
        "decays": jnp.clip(jnp.exp(math.log(0.95) - 2.2512918 * jax.random.uniform(keys[5], (SUBWIN, LEV, NY, LON), jnp.float32) ** shard_levels(keys[5], (SUBWIN, LEV, NY, LON), ((0, 2), (2, 64)), -0.2, 0.2)), 0.1, 0.95),
        "scaling": jnp.clip(jnp.exp(math.log(1.0) - 0.6931472 * jax.random.uniform(keys[6], (LEV, NY, LON), jnp.float32) ** shard_levels(keys[6], (LEV, NY, LON), ((1, 64),), -0.2, 0.2)), 0.5, 1.0),
        "diffusion": jnp.clip(jax.random.uniform(keys[7], (LEV,), jnp.float32, 0.05, 0.24), 0.05, 0.24),
        "owners": draw_owners(jax.random.fold_in(keys[13], 71), 0),
        "tile_cols": draw_tile_cols(jax.random.fold_in(keys[13], 71), 0),
        "jacobian": scatter_about(keys[10], (SUBWIN, TILES, OROWS, TCOLS * LEV), (TCOLS * LEV) ** -0.5, 0.1875, ((0, 2), (1, 64))),
        "innovation": scatter_about(keys[11], (SUBWIN, TILES, OROWS), 1.0, 6.0, ((0, 2), (1, 64))),
        "obs_var": jnp.clip(jnp.exp(math.log(4.0) - 2.0794415 * jax.random.uniform(keys[12], (SUBWIN, TILES, OROWS), jnp.float32) ** shard_levels(keys[12], (SUBWIN, TILES, OROWS), ((0, 2), (1, 64)), -0.2, 0.2)), 0.5, 4.0).astype(jnp.bfloat16),
    }


def model_apply(state_in, scaling, diffusion):
    current = state_in
    for repeat in range(SUBSTEPS):
        scaled = scaling * current
        padded = jnp.pad(scaled, ((0, 0), (1, 1), (0, 0)))
        laplace = padded[:, 2:] + padded[:, :-2] + jnp.roll(scaled, 1, 2) + jnp.roll(scaled, -1, 2) - 4.0 * scaled
        current = scaling * (scaled + diffusion[:, None, None] * laplace)
    return current


def window_model(fields, scaling, diffusion):
    return jax.vmap(model_apply, in_axes=(0, None, None))(fields, scaling, diffusion)


def gather_cells(fields, row_index, col_index):
    window_index = jnp.arange(SUBWIN, dtype=jnp.int32)[:, None, None]
    moved = jnp.transpose(fields, (0, 2, 3, 1))
    picked = moved[window_index, row_index, col_index]
    picked = picked.reshape(SUBWIN, TILES, TCOLS * LEV).astype(jnp.bfloat16)
    return lax.optimization_barrier(picked)


def obs_forward(jacobian, gathered):
    def per_window(operands):
        jac_rows, cells = operands
        return jnp.einsum("toj,tj->to", jac_rows.astype(jnp.float32), cells.astype(jnp.float32))
    return lax.map(per_window, (jacobian, gathered))


def obs_adjoint(jacobian, obs_dual, row_index, col_index):
    rounded = lax.optimization_barrier(obs_dual.astype(jnp.bfloat16))

    def per_window(operands):
        jac_rows, weights = operands
        summed = jnp.einsum("toj,to->tj", jac_rows.astype(jnp.float32), weights.astype(jnp.float32))
        return summed.astype(jnp.bfloat16)
    tile_grad = lax.optimization_barrier(lax.map(per_window, (jacobian, rounded)))
    window_index = jnp.arange(SUBWIN, dtype=jnp.int32)[:, None, None]
    values = tile_grad.astype(jnp.float32).reshape(SUBWIN, TILES, TCOLS, LEV)
    gridded = jnp.zeros((SUBWIN, NY, LON, LEV), jnp.float32).at[window_index, row_index, col_index].add(values)
    return jnp.transpose(gridded, (0, 3, 1, 2))


def reference(increment_start, dual_model_start, dual_obs_start, model_rhs, err_var, decays, scaling, diffusion, owners, tile_cols, jacobian, innovation, obs_var):
    row_index = (owners[:, :, None] * TY + tile_cols // LON).astype(jnp.int32)
    col_index = (tile_cols % LON).astype(jnp.int32)
    observed = innovation.astype(jnp.float32)
    obs_error = obs_var.astype(jnp.float32)
    increment = increment_start
    dual_model = dual_model_start
    obs_dual = dual_obs_start.astype(jnp.float32)
    zero_window = jnp.zeros_like(increment[:1])
    for repeat in range(ITERS):
        forward = jnp.concatenate([zero_window, window_model(increment[:-1], scaling, diffusion)], axis=0)
        backward = jnp.concatenate([window_model(dual_model[1:], scaling, diffusion), zero_window], axis=0)
        obs_image = obs_forward(jacobian, gather_cells(increment, row_index, col_index))
        adjoint_field = obs_adjoint(jacobian, obs_dual, row_index, col_index)
        r_model = model_rhs - err_var * dual_model - (increment - forward)
        r_obs = observed - obs_error * obs_dual - obs_image
        r_dual = -(dual_model - backward) - adjoint_field
        obs_dual = obs_dual + r_obs / obs_error
        carried = r_dual[SUBWIN - 1]
        upward_list = [carried]
        for window in range(SUBWIN - 2, -1, -1):
            carried = r_dual[window] + decays[window + 1] * carried
            upward_list.insert(0, carried)
        upward = jnp.stack(upward_list)
        dual_model = dual_model + upward
        source = r_model - err_var * upward
        carried = source[0]
        along_list = [carried]
        for window in range(1, SUBWIN):
            carried = source[window] + decays[window] * carried
            along_list.append(carried)
        increment = increment + jnp.stack(along_list)
    return dual_model, obs_dual, increment
```

```python
import jax
import jax.numpy as jnp
from jax import lax
from jax.sharding import PartitionSpec as P

SUBSTEPS = 2
ITERS = 2
LANES = 128


def with_halo(cells, axis, dim, width):
    count = lax.axis_size(axis)
    ends = count - 1
    head = lax.slice_in_dim(cells, 0, width, axis=dim)
    tail = lax.slice_in_dim(cells, cells.shape[dim] - width, cells.shape[dim], axis=dim)
    return jnp.concatenate(
        [
            lax.ppermute(tail, axis, [(i, i + 1) for i in range(ends)]),
            cells,
            lax.ppermute(head, axis, [(i + 1, i) for i in range(ends)]),
        ],
        axis=dim,
    )


def shifted(value, axis, by):
    length = lax.axis_size(axis)
    pairs = [(i, i + by) for i in range(length) if 0 <= i + by < length]
    return lax.ppermute(value, axis, pairs)


def model_apply(field, scaling_ext, diff_coef):
    current = with_halo(field, "space", 1, SUBSTEPS)
    for step in range(SUBSTEPS):
        gain = scaling_ext[:, step : scaling_ext.shape[1] - step]
        scaled = gain * current
        inner = scaled[:, 1:-1]
        laplace = (
            scaled[:, 2:]
            + scaled[:, :-2]
            + jnp.roll(inner, 1, 2)
            + jnp.roll(inner, -1, 2)
            - 4.0 * inner
        )
        current = gain[:, 1:-1] * (inner + diff_coef * laplace)
    return current


def gather_cols(fields, row_oh, col_oh, group_mask):
    levels, row_count, col_count = fields.shape
    slots, lanes, touched = col_oh.shape
    groups = col_count // lanes
    lines = jnp.einsum(
        "sr,lrc->slc", row_oh, fields.astype(jnp.bfloat16), preferred_element_type=jnp.float32
    ).astype(jnp.bfloat16)
    lines = lines.reshape(slots, levels, groups, lanes)
    picked = jnp.einsum("slab,sbj->slaj", lines, col_oh, preferred_element_type=jnp.float32)
    picked = jnp.sum(picked * group_mask[:, None, :, :], axis=2)
    return picked.astype(jnp.bfloat16).reshape(slots, levels * touched)


def spread_cols(values, row_oh, col_oh, group_mask, levels, col_count):
    slots, lanes, touched = col_oh.shape
    grads = values.reshape(slots, levels, 1, touched)
    placed = grads * group_mask[:, None, :, :].astype(jnp.bfloat16)
    lines = jnp.einsum("slaj,sbj->slab", placed, col_oh, preferred_element_type=jnp.float32)
    lines = lines.reshape(slots, levels, col_count)
    return jnp.einsum("sr,slc->lrc", row_oh, lines, precision=lax.Precision.HIGHEST)


def on_device(
    increment_start,
    dual_model_start,
    dual_obs_start,
    model_rhs,
    err_var,
    decays,
    scaling,
    diffusion,
    owners,
    tile_cols,
    jacobian,
    innovation,
    obs_var,
):
    increment = increment_start[0]
    dual_model = dual_model_start[0]
    rhs_field = model_rhs[0]
    err_field = err_var[0]
    decay_field = decays[0]
    owner_list = owners[0]
    cell_index = tile_cols[0]
    observed = innovation[0].astype(jnp.float32)
    obs_error = obs_var[0].astype(jnp.float32)
    obs_dual = dual_obs_start[0].astype(jnp.float32)
    levels, row_count, col_count = increment.shape
    tiles_here, orows, touch_levels = jacobian.shape[1:]
    touched = touch_levels // levels
    owners_count = lax.axis_size("space")
    tm_count = lax.axis_size("tm")
    tm_here = lax.axis_index("tm")
    capacity = max(2, 2 * tiles_here // owners_count)
    slots_all = owners_count * capacity
    groups = col_count // LANES
    diff_coef = diffusion[:, None, None]

    jac_tiles = (
        jacobian[0]
        .reshape(tiles_here, orows, touched, levels)
        .transpose(0, 1, 3, 2)
        .reshape(tiles_here, orows, touch_levels)
    )

    one_hot = (owner_list[:, None] == jnp.arange(owners_count, dtype=jnp.int32)[None, :]).astype(
        jnp.int32
    )
    earlier_count = jnp.cumsum(one_hot, axis=0) - one_hot
    slot_rank = jnp.sum(earlier_count * one_hot, axis=1)
    position = owner_list * capacity + slot_rank
    slot_oh = (position[:, None] == jnp.arange(slots_all, dtype=jnp.int32)[None, :]).astype(
        jnp.bfloat16
    )
    packed_cells = jnp.zeros((slots_all, touched), jnp.int32).at[position].set(cell_index)
    requests = lax.all_to_all(
        packed_cells.reshape(owners_count, capacity, touched),
        "space",
        split_axis=0,
        concat_axis=0,
        tiled=True,
    ).reshape(slots_all, touched)
    req_rows = requests[:, 0] // col_count
    req_cols = requests % col_count
    row_oh = (req_rows[:, None] == jnp.arange(row_count, dtype=jnp.int32)[None, :])
    col_oh = (
        (req_cols % LANES)[:, None, :] == jnp.arange(LANES, dtype=jnp.int32)[None, :, None]
    ).astype(jnp.bfloat16)
    group_mask = (
        (req_cols // LANES)[:, None, :] == jnp.arange(groups, dtype=jnp.int32)[None, :, None]
    ).astype(jnp.float32)

    scaling_ext = with_halo(scaling, "space", 1, SUBSTEPS)
    is_first = (tm_here == 0).astype(jnp.float32)
    is_last = (tm_here == tm_count - 1).astype(jnp.float32)

    for repeat in range(ITERS):
        wanted = gather_cols(increment, row_oh.astype(jnp.bfloat16), col_oh, group_mask)
        tile_grad = jnp.einsum(
            "toj,to->tj", jac_tiles, obs_dual.astype(jnp.bfloat16), preferred_element_type=jnp.float32
        ).astype(jnp.bfloat16)
        sent_grad = jnp.einsum(
            "ts,tj->sj", slot_oh, tile_grad, preferred_element_type=jnp.float32
        ).astype(jnp.bfloat16)
        both = jnp.stack(
            [
                wanted.reshape(owners_count, capacity, touch_levels),
                sent_grad.reshape(owners_count, capacity, touch_levels),
            ],
            axis=1,
        )
        got = lax.all_to_all(both, "space", split_axis=0, concat_axis=0, tiled=True)
        got_cols = got[:, 0].reshape(slots_all, touch_levels)
        got_grad = got[:, 1].reshape(slots_all, touch_levels)
        own_cols = jnp.einsum(
            "ts,sj->tj", slot_oh, got_cols, preferred_element_type=jnp.float32
        ).astype(jnp.bfloat16)
        obs_image = jnp.einsum(
            "toj,tj->to", jac_tiles, own_cols, preferred_element_type=jnp.float32
        )
        adjoint_field = spread_cols(
            got_grad, row_oh.astype(jnp.float32), col_oh, group_mask, levels, col_count
        )

        if tm_count == 2:
            chosen = jnp.where(tm_here == 0, increment, dual_model)
            applied = model_apply(chosen, scaling_ext, diff_coef)
            other = lax.ppermute(applied, "tm", [(0, 1), (1, 0)])
            forward = other * (1.0 - is_first)
            backward = other * (1.0 - is_last)
        else:
            applied = model_apply(jnp.stack([increment, dual_model]).reshape(2 * levels, row_count, col_count),
                                  jnp.concatenate([scaling_ext, scaling_ext]), jnp.concatenate([diff_coef, diff_coef]))
            forward = shifted(applied[:levels], "tm", 1)
            backward = shifted(applied[levels:], "tm", -1)

        obs_dual = obs_dual + (observed - obs_error * obs_dual - obs_image) / obs_error
        r_model = rhs_field - err_field * dual_model - (increment - forward)
        r_dual = -(dual_model - backward) - adjoint_field
        upward = r_dual
        upward = r_dual + shifted(decay_field * upward, "tm", -1)
        source = r_model - err_field * upward
        along = source
        along = source + decay_field * shifted(along, "tm", 1)
        dual_model = dual_model + upward
        increment = increment + along
    return (dual_model[None], obs_dual[None], increment[None])


def solution(mesh):
    in_specs = (
        P("tm", None, "space", None),
        P("tm", None, "space", None),
        P("tm", "space", None),
        P("tm", None, "space", None),
        P("tm", None, "space", None),
        P("tm", None, "space", None),
        P(None, "space", None),
        P(),
        P("tm", "space"),
        P("tm", "space", None),
        P("tm", "space", None, None),
        P("tm", "space", None),
        P("tm", "space", None),
    )
    out_specs = (P("tm", None, "space", None), P("tm", "space", None), P("tm", None, "space", None))
    return jax.shard_map(
        on_device, mesh=mesh, in_specs=in_specs, out_specs=out_specs, check_vma=False
    )
```

```python
import jax
import jax.numpy as jnp
from jax import lax
from jax.sharding import PartitionSpec as P

SUBSTEPS = 2
ITERS = 2
LANES = 128


def with_halo(cells, axis, dim, width):
    count = lax.axis_size(axis)
    ends = count - 1
    head = lax.slice_in_dim(cells, 0, width, axis=dim)
    tail = lax.slice_in_dim(cells, cells.shape[dim] - width, cells.shape[dim], axis=dim)
    return jnp.concatenate(
        [
            lax.ppermute(tail, axis, [(i, i + 1) for i in range(ends)]),
            cells,
            lax.ppermute(head, axis, [(i + 1, i) for i in range(ends)]),
        ],
        axis=dim,
    )


def shifted(value, axis, by):
    length = lax.axis_size(axis)
    pairs = [(i, i + by) for i in range(length) if 0 <= i + by < length]
    return lax.ppermute(value, axis, pairs)


def model_apply(field, scaling_ext, diff_coef):
    current = with_halo(field, "space", 1, SUBSTEPS)
    for step in range(SUBSTEPS):
        gain = scaling_ext[:, step : scaling_ext.shape[1] - step]
        scaled = gain * current
        inner = scaled[:, 1:-1]
        laplace = (
            scaled[:, 2:]
            + scaled[:, :-2]
            + jnp.roll(inner, 1, 2)
            + jnp.roll(inner, -1, 2)
            - 4.0 * inner
        )
        current = gain[:, 1:-1] * (inner + diff_coef * laplace)
    return current


def gather_cols(fields, row_oh, col_oh, group_mask):
    levels, row_count, col_count = fields.shape
    slots, lanes, touched = col_oh.shape
    groups = col_count // lanes
    lines = jnp.einsum(
        "sr,lrc->slc", row_oh, fields.astype(jnp.bfloat16), preferred_element_type=jnp.float32
    ).astype(jnp.bfloat16)
    lines = lines.reshape(slots, levels, groups, lanes)
    picked = jnp.einsum("slab,sbj->slaj", lines, col_oh, preferred_element_type=jnp.float32)
    picked = jnp.sum(picked * group_mask[:, None, :, :], axis=2)
    return picked.astype(jnp.bfloat16).reshape(slots, levels * touched)


def spread_cols(values, row_oh, col_oh, group_mask, levels, col_count):
    slots, lanes, touched = col_oh.shape
    groups = col_count // lanes
    row_count = row_oh.shape[1]
    grads = values.reshape(slots, levels, 1, touched)
    placed = grads * group_mask[:, None, :, :].astype(jnp.bfloat16)
    lines = jnp.einsum("slaj,sbj->slab", placed, col_oh, preferred_element_type=jnp.float32)
    high = lines.astype(jnp.bfloat16)
    low = (lines - high.astype(jnp.float32)).astype(jnp.bfloat16)
    total = jnp.einsum(
        "sr,slab->lrab", row_oh, high, preferred_element_type=jnp.float32
    ) + jnp.einsum("sr,slab->lrab", row_oh, low, preferred_element_type=jnp.float32)
    return total.reshape(levels, row_count, groups * lanes)


def on_device(
    increment_start,
    dual_model_start,
    dual_obs_start,
    model_rhs,
    err_var,
    decays,
    scaling,
    diffusion,
    owners,
    tile_cols,
    jacobian,
    innovation,
    obs_var,
):
    increment = increment_start[0]
    dual_model = dual_model_start[0]
    rhs_field = model_rhs[0]
    err_field = err_var[0]
    decay_field = decays[0]
    owner_list = owners[0]
    cell_index = tile_cols[0]
    observed = innovation[0].astype(jnp.float32)
    obs_error = obs_var[0].astype(jnp.float32)
    obs_dual = dual_obs_start[0].astype(jnp.float32)
    levels, row_count, col_count = increment.shape
    tiles_here, orows, touch_levels = jacobian.shape[1:]
    touched = touch_levels // levels
    owners_count = lax.axis_size("space")
    tm_count = lax.axis_size("tm")
    tm_here = lax.axis_index("tm")
    capacity = max(2, 2 * tiles_here // owners_count)
    slots_all = owners_count * capacity
    groups = col_count // LANES
    diff_coef = diffusion[:, None, None]

    jac_tiles = jacobian[0]

    one_hot = (owner_list[:, None] == jnp.arange(owners_count, dtype=jnp.int32)[None, :]).astype(
        jnp.int32
    )
    earlier_count = jnp.cumsum(one_hot, axis=0) - one_hot
    slot_rank = jnp.sum(earlier_count * one_hot, axis=1)
    position = owner_list * capacity + slot_rank
    slot_oh = (position[:, None] == jnp.arange(slots_all, dtype=jnp.int32)[None, :]).astype(
        jnp.bfloat16
    )
    packed_cells = jnp.zeros((slots_all, touched), jnp.int32).at[position].set(cell_index)
    requests = lax.all_to_all(
        packed_cells.reshape(owners_count, capacity, touched),
        "space",
        split_axis=0,
        concat_axis=0,
        tiled=True,
    ).reshape(slots_all, touched)
    req_rows = requests[:, 0] // col_count
    req_cols = requests % col_count
    row_oh = (req_rows[:, None] == jnp.arange(row_count, dtype=jnp.int32)[None, :])
    col_oh = (
        (req_cols % LANES)[:, None, :] == jnp.arange(LANES, dtype=jnp.int32)[None, :, None]
    ).astype(jnp.bfloat16)
    group_mask = (
        (req_cols // LANES)[:, None, :] == jnp.arange(groups, dtype=jnp.int32)[None, :, None]
    ).astype(jnp.float32)

    scaling_ext = with_halo(scaling, "space", 1, SUBSTEPS)
    is_first = (tm_here == 0).astype(jnp.float32)
    is_last = (tm_here == tm_count - 1).astype(jnp.float32)

    for repeat in range(ITERS):
        wanted = gather_cols(increment, row_oh.astype(jnp.bfloat16), col_oh, group_mask)
        tile_grad = jnp.einsum(
            "toj,to->tj", jac_tiles, obs_dual.astype(jnp.bfloat16), preferred_element_type=jnp.float32
        ).astype(jnp.bfloat16)
        sent_grad = jnp.einsum(
            "ts,tjl->slj",
            slot_oh,
            tile_grad.reshape(tiles_here, touched, levels),
            preferred_element_type=jnp.float32,
        ).astype(jnp.bfloat16)
        both = jnp.stack(
            [
                wanted.reshape(owners_count, capacity, touch_levels),
                sent_grad.reshape(owners_count, capacity, touch_levels),
            ],
            axis=1,
        )
        got = lax.all_to_all(both, "space", split_axis=0, concat_axis=0, tiled=True)
        got_cols = got[:, 0].reshape(slots_all, touch_levels)
        got_grad = got[:, 1].reshape(slots_all, touch_levels)
        own_cols = jnp.einsum(
            "ts,slj->tjl",
            slot_oh,
            got_cols.reshape(slots_all, levels, touched),
            preferred_element_type=jnp.float32,
        ).astype(jnp.bfloat16).reshape(tiles_here, touch_levels)
        obs_image = jnp.einsum(
            "toj,tj->to", jac_tiles, own_cols, preferred_element_type=jnp.float32
        )
        adjoint_field = spread_cols(
            got_grad, row_oh.astype(jnp.bfloat16), col_oh, group_mask, levels, col_count
        )

        if tm_count == 2:
            chosen = jnp.where(tm_here == 0, increment, dual_model)
            applied = model_apply(chosen, scaling_ext, diff_coef)
            other = lax.ppermute(applied, "tm", [(0, 1), (1, 0)])
            forward = other * (1.0 - is_first)
            backward = other * (1.0 - is_last)
        else:
            applied = model_apply(jnp.stack([increment, dual_model]).reshape(2 * levels, row_count, col_count),
                                  jnp.concatenate([scaling_ext, scaling_ext]), jnp.concatenate([diff_coef, diff_coef]))
            forward = shifted(applied[:levels], "tm", 1)
            backward = shifted(applied[levels:], "tm", -1)

        obs_dual = obs_dual + (observed - obs_error * obs_dual - obs_image) / obs_error
        r_model = rhs_field - err_field * dual_model - (increment - forward)
        r_dual = -(dual_model - backward) - adjoint_field
        upward = r_dual
        upward = r_dual + shifted(decay_field * upward, "tm", -1)
        source = r_model - err_field * upward
        along = source
        along = source + decay_field * shifted(along, "tm", 1)
        dual_model = dual_model + upward
        increment = increment + along
    return (dual_model[None], obs_dual[None], increment[None])


def solution(mesh):
    in_specs = (
        P("tm", None, "space", None),
        P("tm", None, "space", None),
        P("tm", "space", None),
        P("tm", None, "space", None),
        P("tm", None, "space", None),
        P("tm", None, "space", None),
        P(None, "space", None),
        P(),
        P("tm", "space"),
        P("tm", "space", None),
        P("tm", "space", None, None),
        P("tm", "space", None),
        P("tm", "space", None),
    )
    out_specs = (P("tm", None, "space", None), P("tm", "space", None), P("tm", None, "space", None))
    return jax.shard_map(
        on_device, mesh=mesh, in_specs=in_specs, out_specs=out_specs, check_vma=False
    )
```

```python
import jax
import jax.numpy as jnp
from jax import lax
from jax.sharding import PartitionSpec as P

SUBSTEPS = 2
ITERS = 2
LANES = 128


def with_halo(cells, axis, dim, width):
    count = lax.axis_size(axis)
    ends = count - 1
    head = lax.slice_in_dim(cells, 0, width, axis=dim)
    tail = lax.slice_in_dim(cells, cells.shape[dim] - width, cells.shape[dim], axis=dim)
    return jnp.concatenate(
        [
            lax.ppermute(tail, axis, [(i, i + 1) for i in range(ends)]),
            cells,
            lax.ppermute(head, axis, [(i + 1, i) for i in range(ends)]),
        ],
        axis=dim,
    )


def shifted(value, axis, by):
    length = lax.axis_size(axis)
    pairs = [(i, i + by) for i in range(length) if 0 <= i + by < length]
    return lax.ppermute(value, axis, pairs)


def model_apply(field, scaling_ext, diff_coef):
    current = with_halo(field, "space", 1, SUBSTEPS)
    for step in range(SUBSTEPS):
        gain = scaling_ext[:, step : scaling_ext.shape[1] - step]
        scaled = gain * current
        inner = scaled[:, 1:-1]
        laplace = (
            scaled[:, 2:]
            + scaled[:, :-2]
            + jnp.roll(inner, 1, 2)
            + jnp.roll(inner, -1, 2)
            - 4.0 * inner
        )
        current = gain[:, 1:-1] * (inner + diff_coef * laplace)
    return current


def gather_cols(fields, row_oh, col_oh, group_mask):
    levels, row_count, col_count = fields.shape
    slots, lanes, touched = col_oh.shape
    groups = col_count // lanes
    lines = jnp.einsum(
        "sr,lrc->slc", row_oh, fields.astype(jnp.bfloat16), preferred_element_type=jnp.float32
    ).astype(jnp.bfloat16)
    lines = lines.reshape(slots, levels, groups, lanes)
    picked = jnp.einsum("slab,sbj->slaj", lines, col_oh, preferred_element_type=jnp.float32)
    picked = jnp.sum(picked * group_mask[:, None, :, :], axis=2)
    return picked.astype(jnp.bfloat16).reshape(slots, levels * touched)


def spread_cols(values, row_oh, col_oh, group_mask, levels, col_count):
    slots, lanes, touched = col_oh.shape
    groups = col_count // lanes
    row_count = row_oh.shape[1]
    grads = values.reshape(slots, levels, 1, touched)
    placed = grads * group_mask[:, None, :, :].astype(jnp.bfloat16)
    lines = jnp.einsum("slaj,sbj->slab", placed, col_oh, preferred_element_type=jnp.float32)
    high = lax.reduce_precision(lines, exponent_bits=8, mantissa_bits=7)
    low = (lines - high).astype(jnp.bfloat16)
    high = high.astype(jnp.bfloat16)
    total = jnp.einsum(
        "sr,slab->lrab", row_oh, high, preferred_element_type=jnp.float32
    ) + jnp.einsum("sr,slab->lrab", row_oh, low, preferred_element_type=jnp.float32)
    return total.reshape(levels, row_count, groups * lanes)


def on_device(
    increment_start,
    dual_model_start,
    dual_obs_start,
    model_rhs,
    err_var,
    decays,
    scaling,
    diffusion,
    owners,
    tile_cols,
    jacobian,
    innovation,
    obs_var,
):
    increment = increment_start[0]
    dual_model = dual_model_start[0]
    rhs_field = model_rhs[0]
    err_field = err_var[0]
    decay_field = decays[0]
    owner_list = owners[0]
    cell_index = tile_cols[0]
    observed = innovation[0].astype(jnp.float32)
    obs_error = obs_var[0].astype(jnp.float32)
    obs_dual = dual_obs_start[0].astype(jnp.float32)
    levels, row_count, col_count = increment.shape
    tiles_here, orows, touch_levels = jacobian.shape[1:]
    touched = touch_levels // levels
    owners_count = lax.axis_size("space")
    tm_count = lax.axis_size("tm")
    tm_here = lax.axis_index("tm")
    capacity = max(2, 2 * tiles_here // owners_count)
    slots_all = owners_count * capacity
    groups = col_count // LANES
    diff_coef = diffusion[:, None, None]

    jac_tiles = jacobian[0]

    one_hot = (owner_list[:, None] == jnp.arange(owners_count, dtype=jnp.int32)[None, :]).astype(
        jnp.int32
    )
    earlier_count = jnp.cumsum(one_hot, axis=0) - one_hot
    slot_rank = jnp.sum(earlier_count * one_hot, axis=1)
    position = owner_list * capacity + slot_rank
    slot_oh = (position[:, None] == jnp.arange(slots_all, dtype=jnp.int32)[None, :]).astype(
        jnp.bfloat16
    )
    tables = lax.all_gather(
        jnp.concatenate([position[:, None], cell_index], axis=1), "space", axis=0, tiled=False
    )
    slot_ids = lax.axis_index("space") * capacity + jnp.arange(capacity, dtype=jnp.int32)
    match = (tables[:, None, :, 0] == slot_ids[None, :, None]).astype(jnp.int32)
    requests = jnp.sum(match[..., None] * tables[:, None, :, 1:], axis=2).reshape(
        slots_all, touched
    )
    req_rows = requests[:, 0] // col_count
    req_cols = requests % col_count
    row_oh = (req_rows[:, None] == jnp.arange(row_count, dtype=jnp.int32)[None, :])
    col_oh = (
        (req_cols % LANES)[:, None, :] == jnp.arange(LANES, dtype=jnp.int32)[None, :, None]
    ).astype(jnp.bfloat16)
    group_mask = (
        (req_cols // LANES)[:, None, :] == jnp.arange(groups, dtype=jnp.int32)[None, :, None]
    ).astype(jnp.float32)

    scaling_ext = with_halo(scaling, "space", 1, SUBSTEPS)
    is_first = (tm_here == 0).astype(jnp.float32)
    is_last = (tm_here == tm_count - 1).astype(jnp.float32)

    for repeat in range(ITERS):
        wanted = gather_cols(increment, row_oh.astype(jnp.bfloat16), col_oh, group_mask)
        tile_grad = jnp.einsum(
            "toj,to->tj", jac_tiles, obs_dual.astype(jnp.bfloat16), preferred_element_type=jnp.float32
        ).astype(jnp.bfloat16)
        sent_grad = jnp.einsum(
            "ts,tjl->slj",
            slot_oh,
            tile_grad.reshape(tiles_here, touched, levels),
            preferred_element_type=jnp.float32,
        ).astype(jnp.bfloat16)
        both = jnp.stack(
            [
                wanted.reshape(owners_count, capacity, touch_levels),
                sent_grad.reshape(owners_count, capacity, touch_levels),
            ],
            axis=1,
        )
        got = lax.all_to_all(both, "space", split_axis=0, concat_axis=0, tiled=True)
        got_cols = got[:, 0].reshape(slots_all, touch_levels)
        got_grad = got[:, 1].reshape(slots_all, touch_levels)
        own_cols = jnp.einsum(
            "ts,slj->tjl",
            slot_oh,
            got_cols.reshape(slots_all, levels, touched),
            preferred_element_type=jnp.float32,
        ).astype(jnp.bfloat16).reshape(tiles_here, touch_levels)
        obs_image = jnp.einsum(
            "toj,tj->to", jac_tiles, own_cols, preferred_element_type=jnp.float32
        )
        adjoint_field = spread_cols(
            got_grad, row_oh.astype(jnp.bfloat16), col_oh, group_mask, levels, col_count
        )

        if tm_count == 2:
            chosen = jnp.where(tm_here == 0, increment, dual_model)
            applied = model_apply(chosen, scaling_ext, diff_coef)
            other = lax.ppermute(applied, "tm", [(0, 1), (1, 0)])
            forward = other * (1.0 - is_first)
            backward = other * (1.0 - is_last)
        else:
            applied = model_apply(jnp.stack([increment, dual_model]).reshape(2 * levels, row_count, col_count),
                                  jnp.concatenate([scaling_ext, scaling_ext]), jnp.concatenate([diff_coef, diff_coef]))
            forward = shifted(applied[:levels], "tm", 1)
            backward = shifted(applied[levels:], "tm", -1)

        obs_dual = obs_dual + (observed - obs_error * obs_dual - obs_image) / obs_error
        r_model = rhs_field - err_field * dual_model - (increment - forward)
        r_dual = -(dual_model - backward) - adjoint_field
        upward = r_dual
        upward = r_dual + shifted(decay_field * upward, "tm", -1)
        source = r_model - err_field * upward
        along = source
        along = source + decay_field * shifted(along, "tm", 1)
        dual_model = dual_model + upward
        increment = increment + along
    return (dual_model[None], obs_dual[None], increment[None])


def solution(mesh):
    in_specs = (
        P("tm", None, "space", None),
        P("tm", None, "space", None),
        P("tm", "space", None),
        P("tm", None, "space", None),
        P("tm", None, "space", None),
        P("tm", None, "space", None),
        P(None, "space", None),
        P(),
        P("tm", "space"),
        P("tm", "space", None),
        P("tm", "space", None, None),
        P("tm", "space", None),
        P("tm", "space", None),
    )
    out_specs = (P("tm", None, "space", None), P("tm", "space", None), P("tm", None, "space", None))
    return jax.shard_map(
        on_device, mesh=mesh, in_specs=in_specs, out_specs=out_specs, check_vma=False
    )
```

```python
import jax
import jax.numpy as jnp
from jax import lax
from jax.sharding import PartitionSpec as P

SUBSTEPS = 2
ITERS = 2
LANES = 128


def with_halo(cells, axis, dim, width):
    count = lax.axis_size(axis)
    ends = count - 1
    head = lax.slice_in_dim(cells, 0, width, axis=dim)
    tail = lax.slice_in_dim(cells, cells.shape[dim] - width, cells.shape[dim], axis=dim)
    return jnp.concatenate(
        [
            lax.ppermute(tail, axis, [(i, i + 1) for i in range(ends)]),
            cells,
            lax.ppermute(head, axis, [(i + 1, i) for i in range(ends)]),
        ],
        axis=dim,
    )


def shifted(value, axis, by):
    length = lax.axis_size(axis)
    pairs = [(i, i + by) for i in range(length) if 0 <= i + by < length]
    return lax.ppermute(value, axis, pairs)


def model_apply(current, scaling_ext, diff_coef):
    for step in range(SUBSTEPS):
        gain = scaling_ext[:, step : scaling_ext.shape[1] - step]
        scaled = gain * current
        inner = scaled[:, 1:-1]
        laplace = (
            scaled[:, 2:]
            + scaled[:, :-2]
            + jnp.roll(inner, 1, 2)
            + jnp.roll(inner, -1, 2)
            - 4.0 * inner
        )
        current = gain[:, 1:-1] * (inner + diff_coef * laplace)
    return current


def gather_cols(fields, row_oh, col_oh, group_mask):
    levels, row_count, col_count = fields.shape
    slots, lanes, touched = col_oh.shape
    groups = col_count // lanes
    lines = jnp.einsum(
        "sr,lrc->slc", row_oh, fields.astype(jnp.bfloat16), preferred_element_type=jnp.float32
    ).astype(jnp.bfloat16)
    lines = lines.reshape(slots, levels, groups, lanes)
    picked = jnp.einsum("slab,sbj->slaj", lines, col_oh, preferred_element_type=jnp.float32)
    picked = jnp.sum(picked * group_mask[:, None, :, :], axis=2)
    return picked.astype(jnp.bfloat16).reshape(slots, levels * touched)


def spread_cols(values, row_oh, col_oh, group_mask, levels, col_count):
    slots, lanes, touched = col_oh.shape
    groups = col_count // lanes
    row_count = row_oh.shape[1]
    grads = values.reshape(slots, levels, 1, touched)
    placed = grads * group_mask[:, None, :, :].astype(jnp.bfloat16)
    lines = jnp.einsum("slaj,sbj->slab", placed, col_oh, preferred_element_type=jnp.float32)
    high = lax.reduce_precision(lines, exponent_bits=8, mantissa_bits=7)
    low = (lines - high).astype(jnp.bfloat16)
    high = high.astype(jnp.bfloat16)
    total = jnp.einsum(
        "sr,slab->lrab", row_oh, high, preferred_element_type=jnp.float32
    ) + jnp.einsum("sr,slab->lrab", row_oh, low, preferred_element_type=jnp.float32)
    return total.reshape(levels, row_count, groups * lanes)


def on_device(
    increment_start,
    dual_model_start,
    dual_obs_start,
    model_rhs,
    err_var,
    decays,
    scaling,
    diffusion,
    owners,
    tile_cols,
    jacobian,
    innovation,
    obs_var,
):
    increment = increment_start[0]
    dual_model = dual_model_start[0]
    rhs_field = model_rhs[0]
    err_field = err_var[0]
    decay_field = decays[0]
    owner_list = owners[0]
    cell_index = tile_cols[0]
    observed = innovation[0].astype(jnp.float32)
    obs_error = obs_var[0].astype(jnp.float32)
    obs_dual = dual_obs_start[0].astype(jnp.float32)
    levels, row_count, col_count = increment.shape
    tiles_here, orows, touch_levels = jacobian.shape[1:]
    touched = touch_levels // levels
    owners_count = lax.axis_size("space")
    tm_count = lax.axis_size("tm")
    tm_here = lax.axis_index("tm")
    capacity = max(2, 2 * tiles_here // owners_count)
    slots_all = owners_count * capacity
    groups = col_count // LANES
    diff_coef = diffusion[:, None, None]

    jac_tiles = jacobian[0]

    one_hot = (owner_list[:, None] == jnp.arange(owners_count, dtype=jnp.int32)[None, :]).astype(
        jnp.int32
    )
    earlier_count = jnp.cumsum(one_hot, axis=0) - one_hot
    slot_rank = jnp.sum(earlier_count * one_hot, axis=1)
    position = owner_list * capacity + slot_rank
    slot_oh = (position[:, None] == jnp.arange(slots_all, dtype=jnp.int32)[None, :]).astype(
        jnp.bfloat16
    )
    packed_cells = jnp.zeros((slots_all, touched), jnp.int32).at[position].set(cell_index)
    requests = lax.all_to_all(
        packed_cells.reshape(owners_count, capacity, touched),
        "space",
        split_axis=0,
        concat_axis=0,
        tiled=True,
    ).reshape(slots_all, touched)
    req_rows = requests[:, 0] // col_count
    req_cols = requests % col_count
    row_oh = (req_rows[:, None] == jnp.arange(row_count, dtype=jnp.int32)[None, :])
    col_oh = (
        (req_cols % LANES)[:, None, :] == jnp.arange(LANES, dtype=jnp.int32)[None, :, None]
    ).astype(jnp.bfloat16)
    group_mask = (
        (req_cols // LANES)[:, None, :] == jnp.arange(groups, dtype=jnp.int32)[None, :, None]
    ).astype(jnp.float32)

    scaling_ext = None
    is_first = (tm_here == 0).astype(jnp.float32)
    is_last = (tm_here == tm_count - 1).astype(jnp.float32)

    for repeat in range(ITERS):
        wanted = gather_cols(increment, row_oh.astype(jnp.bfloat16), col_oh, group_mask)
        tile_grad = jnp.einsum(
            "toj,to->tj", jac_tiles, obs_dual.astype(jnp.bfloat16), preferred_element_type=jnp.float32
        ).astype(jnp.bfloat16)
        sent_grad = jnp.einsum(
            "ts,tjl->slj",
            slot_oh,
            tile_grad.reshape(tiles_here, touched, levels),
            preferred_element_type=jnp.float32,
        ).astype(jnp.bfloat16)
        both = jnp.stack(
            [
                wanted.reshape(owners_count, capacity, touch_levels),
                sent_grad.reshape(owners_count, capacity, touch_levels),
            ],
            axis=1,
        )
        got = lax.all_to_all(both, "space", split_axis=0, concat_axis=0, tiled=True)
        got_cols = got[:, 0].reshape(slots_all, touch_levels)
        got_grad = got[:, 1].reshape(slots_all, touch_levels)
        own_cols = jnp.einsum(
            "ts,slj->tjl",
            slot_oh,
            got_cols.reshape(slots_all, levels, touched),
            preferred_element_type=jnp.float32,
        ).astype(jnp.bfloat16).reshape(tiles_here, touch_levels)
        obs_image = jnp.einsum(
            "toj,tj->to", jac_tiles, own_cols, preferred_element_type=jnp.float32
        )
        adjoint_field = spread_cols(
            got_grad, row_oh.astype(jnp.bfloat16), col_oh, group_mask, levels, col_count
        )

        if tm_count == 2:
            chosen = jnp.where(tm_here == 0, increment, dual_model)
            if scaling_ext is None:
                both_ext = with_halo(jnp.stack([scaling, chosen]), "space", 2, SUBSTEPS)
                scaling_ext, chosen_ext = both_ext[0], both_ext[1]
            else:
                chosen_ext = with_halo(chosen, "space", 1, SUBSTEPS)
            applied = model_apply(chosen_ext, scaling_ext, diff_coef)
            last_dual = -(dual_model - 0.0) - adjoint_field
            swapped = lax.ppermute(
                jnp.stack([applied, decay_field * last_dual]), "tm", [(0, 1), (1, 0)]
            )
            forward = swapped[0] * (1.0 - is_first)
            backward = swapped[0] * (1.0 - is_last)
            r_dual = jnp.where(is_last > 0, last_dual, -(dual_model - backward) - adjoint_field)
            upward = r_dual + swapped[1] * (1.0 - is_last)
        else:
            if scaling_ext is None:
                scaling_ext = with_halo(scaling, "space", 1, SUBSTEPS)
            stacked = jnp.stack([increment, dual_model]).reshape(2 * levels, row_count, col_count)
            applied = model_apply(
                with_halo(stacked, "space", 1, SUBSTEPS),
                jnp.concatenate([scaling_ext, scaling_ext]),
                jnp.concatenate([diff_coef, diff_coef]),
            )
            forward = shifted(applied[:levels], "tm", 1)
            backward = shifted(applied[levels:], "tm", -1)
            r_dual = -(dual_model - backward) - adjoint_field
            upward = r_dual + shifted(decay_field * r_dual, "tm", -1)

        obs_dual = obs_dual + (observed - obs_error * obs_dual - obs_image) / obs_error
        r_model = rhs_field - err_field * dual_model - (increment - forward)
        source = r_model - err_field * upward
        along = source
        along = source + decay_field * shifted(along, "tm", 1)
        dual_model = dual_model + upward
        increment = increment + along
    return (dual_model[None], obs_dual[None], increment[None])


def solution(mesh):
    in_specs = (
        P("tm", None, "space", None),
        P("tm", None, "space", None),
        P("tm", "space", None),
        P("tm", None, "space", None),
        P("tm", None, "space", None),
        P("tm", None, "space", None),
        P(None, "space", None),
        P(),
        P("tm", "space"),
        P("tm", "space", None),
        P("tm", "space", None, None),
        P("tm", "space", None),
        P("tm", "space", None),
    )
    out_specs = (P("tm", None, "space", None), P("tm", "space", None), P("tm", None, "space", None))
    return jax.shard_map(
        on_device, mesh=mesh, in_specs=in_specs, out_specs=out_specs, check_vma=False
    )
```

```python
import jax
import jax.numpy as jnp
from jax import lax
from jax.sharding import PartitionSpec as P

SUBSTEPS = 2
ITERS = 2
LANES = 128


def with_halo(cells, axis, dim, width):
    count = lax.axis_size(axis)
    ends = count - 1
    head = lax.slice_in_dim(cells, 0, width, axis=dim)
    tail = lax.slice_in_dim(cells, cells.shape[dim] - width, cells.shape[dim], axis=dim)
    return jnp.concatenate(
        [
            lax.ppermute(tail, axis, [(i, i + 1) for i in range(ends)]),
            cells,
            lax.ppermute(head, axis, [(i + 1, i) for i in range(ends)]),
        ],
        axis=dim,
    )


def shifted(value, axis, by):
    length = lax.axis_size(axis)
    pairs = [(i, i + by) for i in range(length) if 0 <= i + by < length]
    return lax.ppermute(value, axis, pairs)


def model_apply(current, scaling_ext, diff_coef):
    for step in range(SUBSTEPS):
        gain = scaling_ext[:, step : scaling_ext.shape[1] - step]
        scaled = gain * current
        inner = scaled[:, 1:-1]
        laplace = (
            scaled[:, 2:]
            + scaled[:, :-2]
            + jnp.roll(inner, 1, 2)
            + jnp.roll(inner, -1, 2)
            - 4.0 * inner
        )
        current = gain[:, 1:-1] * (inner + diff_coef * laplace)
    return current


def gather_cols(fields, row_oh, col_oh, group_mask):
    levels, row_count, col_count = fields.shape
    slots, lanes, touched = col_oh.shape
    groups = col_count // lanes
    lines = jnp.einsum(
        "sr,lrc->slc", row_oh, fields.astype(jnp.bfloat16), preferred_element_type=jnp.float32
    ).astype(jnp.bfloat16)
    lines = lines.reshape(slots, levels, groups, lanes)
    picked = jnp.einsum("slab,sbj->slaj", lines, col_oh, preferred_element_type=jnp.float32)
    picked = jnp.sum(picked * group_mask[:, None, :, :], axis=2)
    return picked.astype(jnp.bfloat16).reshape(slots, levels * touched)


def spread_cols(values, row_oh, col_oh, group_mask, levels, col_count):
    slots, lanes, touched = col_oh.shape
    groups = col_count // lanes
    row_count = row_oh.shape[1]
    grads = values.reshape(slots, levels, 1, touched)
    placed = grads * group_mask[:, None, :, :].astype(jnp.bfloat16)
    lines = jnp.einsum("slaj,sbj->slab", placed, col_oh, preferred_element_type=jnp.float32)
    high = lax.reduce_precision(lines, exponent_bits=8, mantissa_bits=7)
    low = (lines - high).astype(jnp.bfloat16)
    high = high.astype(jnp.bfloat16)
    total = jnp.einsum(
        "sr,slab->lrab", row_oh, high, preferred_element_type=jnp.float32
    ) + jnp.einsum("sr,slab->lrab", row_oh, low, preferred_element_type=jnp.float32)
    return total.reshape(levels, row_count, groups * lanes)


def on_device(
    increment_start,
    dual_model_start,
    dual_obs_start,
    model_rhs,
    err_var,
    decays,
    scaling,
    diffusion,
    owners,
    tile_cols,
    jacobian,
    innovation,
    obs_var,
):
    increment = increment_start[0]
    dual_model = dual_model_start[0]
    rhs_field = model_rhs[0]
    err_field = err_var[0]
    decay_field = decays[0]
    owner_list = owners[0]
    cell_index = tile_cols[0]
    observed = innovation[0].astype(jnp.float32)
    obs_error = obs_var[0].astype(jnp.float32)
    obs_dual = dual_obs_start[0].astype(jnp.float32)
    levels, row_count, col_count = increment.shape
    tiles_here, orows, touch_levels = jacobian.shape[1:]
    touched = touch_levels // levels
    owners_count = lax.axis_size("space")
    tm_count = lax.axis_size("tm")
    tm_here = lax.axis_index("tm")
    capacity = max(2, 2 * tiles_here // owners_count)
    slots_all = owners_count * capacity
    groups = col_count // LANES
    diff_coef = diffusion[:, None, None]

    jac_tiles = jacobian[0]

    one_hot = (owner_list[:, None] == jnp.arange(owners_count, dtype=jnp.int32)[None, :]).astype(
        jnp.int32
    )
    earlier_count = jnp.cumsum(one_hot, axis=0) - one_hot
    slot_rank = jnp.sum(earlier_count * one_hot, axis=1)
    position = owner_list * capacity + slot_rank
    slot_oh = (position[:, None] == jnp.arange(slots_all, dtype=jnp.int32)[None, :]).astype(
        jnp.bfloat16
    )
    packed_cells = jnp.zeros((slots_all, touched), jnp.int32).at[position].set(cell_index)
    requests = lax.all_to_all(
        packed_cells.reshape(owners_count, capacity, touched),
        "space",
        split_axis=0,
        concat_axis=0,
        tiled=True,
    ).reshape(slots_all, touched)
    req_rows = requests[:, 0] // col_count
    req_cols = requests % col_count
    row_oh = (req_rows[:, None] == jnp.arange(row_count, dtype=jnp.int32)[None, :])
    col_oh = (
        (req_cols % LANES)[:, None, :] == jnp.arange(LANES, dtype=jnp.int32)[None, :, None]
    ).astype(jnp.bfloat16)
    group_mask = (
        (req_cols // LANES)[:, None, :] == jnp.arange(groups, dtype=jnp.int32)[None, :, None]
    ).astype(jnp.float32)

    scaling_ext = None
    is_first = (tm_here == 0).astype(jnp.float32)
    is_last = (tm_here == tm_count - 1).astype(jnp.float32)

    for repeat in range(ITERS):
        wanted = gather_cols(increment, row_oh.astype(jnp.bfloat16), col_oh, group_mask)
        tile_grad = jnp.einsum(
            "toj,to->tj", jac_tiles, obs_dual.astype(jnp.bfloat16), preferred_element_type=jnp.float32
        ).astype(jnp.bfloat16)
        sent_grad = jnp.einsum(
            "ts,tjl->slj",
            slot_oh,
            tile_grad.reshape(tiles_here, touched, levels),
            preferred_element_type=jnp.float32,
        ).astype(jnp.bfloat16)
        both = jnp.stack(
            [
                wanted.reshape(owners_count, capacity, touch_levels),
                sent_grad.reshape(owners_count, capacity, touch_levels),
            ],
            axis=1,
        )
        got = lax.all_to_all(both, "space", split_axis=0, concat_axis=0, tiled=True)
        got_cols = got[:, 0].reshape(slots_all, touch_levels)
        got_grad = got[:, 1].reshape(slots_all, touch_levels)
        own_cols = jnp.einsum(
            "ts,slj->tjl",
            slot_oh,
            got_cols.reshape(slots_all, levels, touched),
            preferred_element_type=jnp.float32,
        ).astype(jnp.bfloat16).reshape(tiles_here, touch_levels)
        obs_image = jnp.einsum(
            "toj,tj->to", jac_tiles, own_cols, preferred_element_type=jnp.float32
        )
        adjoint_field = spread_cols(
            got_grad, row_oh.astype(jnp.bfloat16), col_oh, group_mask, levels, col_count
        )

        if tm_count == 2:
            chosen = jnp.where(tm_here == 0, increment, dual_model)
            if scaling_ext is None:
                both_ext = with_halo(jnp.stack([scaling, chosen]), "space", 2, SUBSTEPS)
                scaling_ext, chosen_ext = both_ext[0], both_ext[1]
            else:
                chosen_ext = with_halo(chosen, "space", 1, SUBSTEPS)
            applied = model_apply(chosen_ext, scaling_ext, diff_coef)
            other = lax.ppermute(applied, "tm", [(0, 1), (1, 0)])
            forward = other * (1.0 - is_first)
            backward = other * (1.0 - is_last)
            r_dual = -(dual_model - backward) - adjoint_field
            upward = r_dual + shifted(decay_field * r_dual, "tm", -1)
        else:
            if scaling_ext is None:
                scaling_ext = with_halo(scaling, "space", 1, SUBSTEPS)
            stacked = jnp.stack([increment, dual_model]).reshape(2 * levels, row_count, col_count)
            applied = model_apply(
                with_halo(stacked, "space", 1, SUBSTEPS),
                jnp.concatenate([scaling_ext, scaling_ext]),
                jnp.concatenate([diff_coef, diff_coef]),
            )
            forward = shifted(applied[:levels], "tm", 1)
            backward = shifted(applied[levels:], "tm", -1)
            r_dual = -(dual_model - backward) - adjoint_field
            upward = r_dual + shifted(decay_field * r_dual, "tm", -1)

        obs_dual = obs_dual + (observed - obs_error * obs_dual - obs_image) / obs_error
        r_model = rhs_field - err_field * dual_model - (increment - forward)
        source = r_model - err_field * upward
        along = source
        along = source + decay_field * shifted(along, "tm", 1)
        dual_model = dual_model + upward
        increment = increment + along
    return (dual_model[None], obs_dual[None], increment[None])


def solution(mesh):
    in_specs = (
        P("tm", None, "space", None),
        P("tm", None, "space", None),
        P("tm", "space", None),
        P("tm", None, "space", None),
        P("tm", None, "space", None),
        P("tm", None, "space", None),
        P(None, "space", None),
        P(),
        P("tm", "space"),
        P("tm", "space", None),
        P("tm", "space", None, None),
        P("tm", "space", None),
        P("tm", "space", None),
    )
    out_specs = (P("tm", None, "space", None), P("tm", "space", None), P("tm", None, "space", None))
    return jax.shard_map(
        on_device, mesh=mesh, in_specs=in_specs, out_specs=out_specs, check_vma=False
    )
```

```python
import jax
import jax.numpy as jnp
from jax import lax
from jax.sharding import PartitionSpec as P

SUBSTEPS = 2
ITERS = 2
LANES = 128


def with_halo(cells, axis, dim, width):
    count = lax.axis_size(axis)
    ends = count - 1
    head = lax.slice_in_dim(cells, 0, width, axis=dim)
    tail = lax.slice_in_dim(cells, cells.shape[dim] - width, cells.shape[dim], axis=dim)
    return jnp.concatenate(
        [
            lax.ppermute(tail, axis, [(i, i + 1) for i in range(ends)]),
            cells,
            lax.ppermute(head, axis, [(i + 1, i) for i in range(ends)]),
        ],
        axis=dim,
    )


def shifted(value, axis, by):
    length = lax.axis_size(axis)
    pairs = [(i, i + by) for i in range(length) if 0 <= i + by < length]
    return lax.ppermute(value, axis, pairs)


def model_apply(current, scaling_ext, diff_coef):
    for step in range(SUBSTEPS):
        gain = scaling_ext[:, step : scaling_ext.shape[1] - step]
        scaled = gain * current
        inner = scaled[:, 1:-1]
        laplace = (
            scaled[:, 2:]
            + scaled[:, :-2]
            + jnp.roll(inner, 1, 2)
            + jnp.roll(inner, -1, 2)
            - 4.0 * inner
        )
        current = gain[:, 1:-1] * (inner + diff_coef * laplace)
    return current


def gather_cols(fields, row_oh, col_oh, group_mask):
    levels, row_count, col_count = fields.shape
    slots, lanes, touched = col_oh.shape
    groups = col_count // lanes
    lines = jnp.einsum(
        "sr,lrc->slc", row_oh, fields.astype(jnp.bfloat16), preferred_element_type=jnp.float32
    ).astype(jnp.bfloat16)
    lines = lines.reshape(slots, levels, groups, lanes)
    picked = jnp.einsum("slab,sbj->slaj", lines, col_oh, preferred_element_type=jnp.float32)
    picked = jnp.sum(picked * group_mask[:, None, :, :], axis=2)
    return picked.astype(jnp.bfloat16).reshape(slots, levels * touched)


def spread_cols(values, row_oh, col_oh, group_mask, levels, col_count):
    slots, lanes, touched = col_oh.shape
    groups = col_count // lanes
    row_count = row_oh.shape[1]
    grads = values.reshape(slots, levels, 1, touched)
    placed = grads * group_mask[:, None, :, :].astype(jnp.bfloat16)
    lines = jnp.einsum("slaj,sbj->slab", placed, col_oh, preferred_element_type=jnp.float32)
    high = lax.reduce_precision(lines, exponent_bits=8, mantissa_bits=7)
    low = (lines - high).astype(jnp.bfloat16)
    high = high.astype(jnp.bfloat16)
    total = jnp.einsum(
        "sr,slab->lrab", row_oh, high, preferred_element_type=jnp.float32
    ) + jnp.einsum("sr,slab->lrab", row_oh, low, preferred_element_type=jnp.float32)
    return total.reshape(levels, row_count, groups * lanes)


def on_device(
    increment_start,
    dual_model_start,
    dual_obs_start,
    model_rhs,
    err_var,
    decays,
    scaling,
    diffusion,
    owners,
    tile_cols,
    jacobian,
    innovation,
    obs_var,
):
    increment = increment_start[0]
    dual_model = dual_model_start[0]
    rhs_field = model_rhs[0]
    err_field = err_var[0]
    decay_field = decays[0]
    owner_list = owners[0]
    cell_index = tile_cols[0]
    observed = innovation[0].astype(jnp.float32)
    obs_error = obs_var[0].astype(jnp.float32)
    obs_dual = dual_obs_start[0].astype(jnp.float32)
    levels, row_count, col_count = increment.shape
    tiles_here, orows, touch_levels = jacobian.shape[1:]
    touched = touch_levels // levels
    owners_count = lax.axis_size("space")
    tm_count = lax.axis_size("tm")
    tm_here = lax.axis_index("tm")
    capacity = max(2, 2 * tiles_here // owners_count)
    slots_all = owners_count * capacity
    groups = col_count // LANES
    diff_coef = diffusion[:, None, None]

    jac_tiles = jacobian[0]

    one_hot = (owner_list[:, None] == jnp.arange(owners_count, dtype=jnp.int32)[None, :]).astype(
        jnp.int32
    )
    earlier_count = jnp.cumsum(one_hot, axis=0) - one_hot
    slot_rank = jnp.sum(earlier_count * one_hot, axis=1)
    position = owner_list * capacity + slot_rank
    slot_oh = (position[:, None] == jnp.arange(slots_all, dtype=jnp.int32)[None, :]).astype(
        jnp.bfloat16
    )
    packed_cells = jnp.zeros((slots_all, touched), jnp.int32).at[position].set(cell_index)
    requests = lax.all_to_all(
        packed_cells.reshape(owners_count, capacity, touched),
        "space",
        split_axis=0,
        concat_axis=0,
        tiled=True,
    ).reshape(slots_all, touched)
    req_rows = requests[:, 0] // col_count
    req_cols = requests % col_count
    row_oh = (req_rows[:, None] == jnp.arange(row_count, dtype=jnp.int32)[None, :])
    col_oh = (
        (req_cols % LANES)[:, None, :] == jnp.arange(LANES, dtype=jnp.int32)[None, :, None]
    ).astype(jnp.bfloat16)
    group_mask = (
        (req_cols // LANES)[:, None, :] == jnp.arange(groups, dtype=jnp.int32)[None, :, None]
    ).astype(jnp.float32)

    scaling_ext = None
    err_prev = shifted(err_field, "tm", 1) if tm_count == 2 else None
    is_first = (tm_here == 0).astype(jnp.float32)
    is_last = (tm_here == tm_count - 1).astype(jnp.float32)

    for repeat in range(ITERS):
        wanted = gather_cols(increment, row_oh.astype(jnp.bfloat16), col_oh, group_mask)
        tile_grad = jnp.einsum(
            "toj,to->tj", jac_tiles, obs_dual.astype(jnp.bfloat16), preferred_element_type=jnp.float32
        ).astype(jnp.bfloat16)
        sent_grad = jnp.einsum(
            "ts,tjl->slj",
            slot_oh,
            tile_grad.reshape(tiles_here, touched, levels),
            preferred_element_type=jnp.float32,
        ).astype(jnp.bfloat16)
        both = jnp.stack(
            [
                wanted.reshape(owners_count, capacity, touch_levels),
                sent_grad.reshape(owners_count, capacity, touch_levels),
            ],
            axis=1,
        )
        got = lax.all_to_all(both, "space", split_axis=0, concat_axis=0, tiled=True)
        got_cols = got[:, 0].reshape(slots_all, touch_levels)
        got_grad = got[:, 1].reshape(slots_all, touch_levels)
        own_cols = jnp.einsum(
            "ts,slj->tjl",
            slot_oh,
            got_cols.reshape(slots_all, levels, touched),
            preferred_element_type=jnp.float32,
        ).astype(jnp.bfloat16).reshape(tiles_here, touch_levels)
        obs_image = jnp.einsum(
            "toj,tj->to", jac_tiles, own_cols, preferred_element_type=jnp.float32
        )
        adjoint_field = spread_cols(
            got_grad, row_oh.astype(jnp.bfloat16), col_oh, group_mask, levels, col_count
        )

        if tm_count == 2:
            chosen = jnp.where(tm_here == 0, increment, dual_model)
            if scaling_ext is None:
                both_ext = with_halo(jnp.stack([scaling, chosen]), "space", 2, SUBSTEPS)
                scaling_ext, chosen_ext = both_ext[0], both_ext[1]
            else:
                chosen_ext = with_halo(chosen, "space", 1, SUBSTEPS)
            applied = model_apply(chosen_ext, scaling_ext, diff_coef)
            other = lax.ppermute(applied, "tm", [(0, 1), (1, 0)])
            forward = other * (1.0 - is_first)
            backward = other * (1.0 - is_last)
            r_dual = -(dual_model - backward) - adjoint_field
            r_model = rhs_field - err_field * dual_model - (increment - forward)
            from_prev = shifted(jnp.stack([r_model, r_dual]), "tm", 1)
            upward = r_dual + shifted(decay_field * r_dual, "tm", -1)
            source = r_model - err_field * upward
            prev_upward = from_prev[1] + decay_field * r_dual
            prev_along = from_prev[0] - err_prev * prev_upward
            along = source + decay_field * prev_along
        else:
            if scaling_ext is None:
                scaling_ext = with_halo(scaling, "space", 1, SUBSTEPS)
            stacked = jnp.stack([increment, dual_model]).reshape(2 * levels, row_count, col_count)
            applied = model_apply(
                with_halo(stacked, "space", 1, SUBSTEPS),
                jnp.concatenate([scaling_ext, scaling_ext]),
                jnp.concatenate([diff_coef, diff_coef]),
            )
            forward = shifted(applied[:levels], "tm", 1)
            backward = shifted(applied[levels:], "tm", -1)
            r_dual = -(dual_model - backward) - adjoint_field
            upward = r_dual + shifted(decay_field * r_dual, "tm", -1)
            r_model = rhs_field - err_field * dual_model - (increment - forward)
            source = r_model - err_field * upward
            along = source
            along = source + decay_field * shifted(along, "tm", 1)

        obs_dual = obs_dual + (observed - obs_error * obs_dual - obs_image) / obs_error
        dual_model = dual_model + upward
        increment = increment + along
    return (dual_model[None], obs_dual[None], increment[None])


def solution(mesh):
    in_specs = (
        P("tm", None, "space", None),
        P("tm", None, "space", None),
        P("tm", "space", None),
        P("tm", None, "space", None),
        P("tm", None, "space", None),
        P("tm", None, "space", None),
        P(None, "space", None),
        P(),
        P("tm", "space"),
        P("tm", "space", None),
        P("tm", "space", None, None),
        P("tm", "space", None),
        P("tm", "space", None),
    )
    out_specs = (P("tm", None, "space", None), P("tm", "space", None), P("tm", None, "space", None))
    return jax.shard_map(
        on_device, mesh=mesh, in_specs=in_specs, out_specs=out_specs, check_vma=False
    )
```

```python
import jax
import jax.numpy as jnp
from jax import lax
from jax.sharding import PartitionSpec as P

SUBSTEPS = 2
ITERS = 2
LANES = 128


def with_halo(cells, axis, dim, width):
    count = lax.axis_size(axis)
    ends = count - 1
    head = lax.slice_in_dim(cells, 0, width, axis=dim)
    tail = lax.slice_in_dim(cells, cells.shape[dim] - width, cells.shape[dim], axis=dim)
    return jnp.concatenate(
        [
            lax.ppermute(tail, axis, [(i, i + 1) for i in range(ends)]),
            cells,
            lax.ppermute(head, axis, [(i + 1, i) for i in range(ends)]),
        ],
        axis=dim,
    )


def shifted(value, axis, by):
    length = lax.axis_size(axis)
    pairs = [(i, i + by) for i in range(length) if 0 <= i + by < length]
    return lax.ppermute(value, axis, pairs)


def model_apply(current, scaling_ext, diff_coef):
    for step in range(SUBSTEPS):
        gain = scaling_ext[:, step : scaling_ext.shape[1] - step]
        scaled = gain * current
        inner = scaled[:, 1:-1]
        laplace = (
            scaled[:, 2:]
            + scaled[:, :-2]
            + jnp.roll(inner, 1, 2)
            + jnp.roll(inner, -1, 2)
            - 4.0 * inner
        )
        current = gain[:, 1:-1] * (inner + diff_coef * laplace)
    return current


def gather_cols(fields, row_oh, col_oh, group_mask):
    levels, row_count, col_count = fields.shape
    slots, lanes, touched = col_oh.shape
    groups = col_count // lanes
    lines = jnp.einsum(
        "sr,lrc->slc", row_oh, fields.astype(jnp.bfloat16), preferred_element_type=jnp.float32
    ).astype(jnp.bfloat16)
    lines = lines.reshape(slots, levels, groups, lanes)
    picked = jnp.einsum("slab,sbj->slaj", lines, col_oh, preferred_element_type=jnp.float32)
    picked = jnp.sum(picked * group_mask[:, None, :, :], axis=2)
    return picked.astype(jnp.bfloat16).reshape(slots, levels * touched)


def spread_cols(values, row_oh, col_oh, group_mask, levels, col_count):
    slots, lanes, touched = col_oh.shape
    groups = col_count // lanes
    row_count = row_oh.shape[1]
    grads = values.reshape(slots, levels, 1, touched)
    placed = grads * group_mask[:, None, :, :].astype(jnp.bfloat16)
    lines = jnp.einsum("slaj,sbj->slab", placed, col_oh, preferred_element_type=jnp.float32)
    high = lax.reduce_precision(lines, exponent_bits=8, mantissa_bits=7)
    low = (lines - high).astype(jnp.bfloat16)
    high = high.astype(jnp.bfloat16)
    total = jnp.einsum(
        "sr,slab->lrab", row_oh, high, preferred_element_type=jnp.float32
    ) + jnp.einsum("sr,slab->lrab", row_oh, low, preferred_element_type=jnp.float32)
    return total.reshape(levels, row_count, groups * lanes)


def on_device(
    increment_start,
    dual_model_start,
    dual_obs_start,
    model_rhs,
    err_var,
    decays,
    scaling,
    diffusion,
    owners,
    tile_cols,
    jacobian,
    innovation,
    obs_var,
):
    increment = increment_start[0]
    dual_model = dual_model_start[0]
    rhs_field = model_rhs[0]
    err_field = err_var[0]
    decay_field = decays[0]
    owner_list = owners[0]
    cell_index = tile_cols[0]
    observed = innovation[0].astype(jnp.float32)
    obs_error = obs_var[0].astype(jnp.float32)
    obs_dual = dual_obs_start[0].astype(jnp.float32)
    levels, row_count, col_count = increment.shape
    tiles_here, orows, touch_levels = jacobian.shape[1:]
    touched = touch_levels // levels
    owners_count = lax.axis_size("space")
    tm_count = lax.axis_size("tm")
    tm_here = lax.axis_index("tm")
    capacity = max(2, 2 * tiles_here // owners_count)
    slots_all = owners_count * capacity
    groups = col_count // LANES
    diff_coef = diffusion[:, None, None]

    jac_tiles = jacobian[0]

    one_hot = (owner_list[:, None] == jnp.arange(owners_count, dtype=jnp.int32)[None, :]).astype(
        jnp.int32
    )
    earlier_count = jnp.cumsum(one_hot, axis=0) - one_hot
    slot_rank = jnp.sum(earlier_count * one_hot, axis=1)
    position = owner_list * capacity + slot_rank
    slot_oh = (position[:, None] == jnp.arange(slots_all, dtype=jnp.int32)[None, :]).astype(
        jnp.bfloat16
    )
    packed_cells = jnp.zeros((slots_all, touched), jnp.int32).at[position].set(cell_index)
    requests = lax.all_to_all(
        packed_cells.reshape(owners_count, capacity, touched),
        "space",
        split_axis=0,
        concat_axis=0,
        tiled=True,
    ).reshape(slots_all, touched)
    req_rows = requests[:, 0] // col_count
    req_cols = requests % col_count
    row_oh = (req_rows[:, None] == jnp.arange(row_count, dtype=jnp.int32)[None, :])
    col_oh = (
        (req_cols % LANES)[:, None, :] == jnp.arange(LANES, dtype=jnp.int32)[None, :, None]
    ).astype(jnp.bfloat16)
    group_mask = (
        (req_cols // LANES)[:, None, :] == jnp.arange(groups, dtype=jnp.int32)[None, :, None]
    ).astype(jnp.float32)

    is_first = (tm_here == 0).astype(jnp.float32)
    is_last = (tm_here == tm_count - 1).astype(jnp.float32)

    scaling_ext = with_halo(scaling, "space", 1, SUBSTEPS)

    def iteration(repeat, carry):
        increment, dual_model, obs_dual = carry
        wanted = gather_cols(increment, row_oh.astype(jnp.bfloat16), col_oh, group_mask)
        tile_grad = jnp.einsum(
            "toj,to->tj", jac_tiles, obs_dual.astype(jnp.bfloat16), preferred_element_type=jnp.float32
        ).astype(jnp.bfloat16)
        sent_grad = jnp.einsum(
            "ts,tjl->slj",
            slot_oh,
            tile_grad.reshape(tiles_here, touched, levels),
            preferred_element_type=jnp.float32,
        ).astype(jnp.bfloat16)
        both = jnp.stack(
            [
                wanted.reshape(owners_count, capacity, touch_levels),
                sent_grad.reshape(owners_count, capacity, touch_levels),
            ],
            axis=1,
        )
        got = lax.all_to_all(both, "space", split_axis=0, concat_axis=0, tiled=True)
        got_cols = got[:, 0].reshape(slots_all, touch_levels)
        got_grad = got[:, 1].reshape(slots_all, touch_levels)
        own_cols = jnp.einsum(
            "ts,slj->tjl",
            slot_oh,
            got_cols.reshape(slots_all, levels, touched),
            preferred_element_type=jnp.float32,
        ).astype(jnp.bfloat16).reshape(tiles_here, touch_levels)
        obs_image = jnp.einsum(
            "toj,tj->to", jac_tiles, own_cols, preferred_element_type=jnp.float32
        )
        adjoint_field = spread_cols(
            got_grad, row_oh.astype(jnp.bfloat16), col_oh, group_mask, levels, col_count
        )

        if tm_count == 2:
            chosen = jnp.where(tm_here == 0, increment, dual_model)
            chosen_ext = with_halo(chosen, "space", 1, SUBSTEPS)
            applied = model_apply(chosen_ext, scaling_ext, diff_coef)
            other = lax.ppermute(applied, "tm", [(0, 1), (1, 0)])
            forward = other * (1.0 - is_first)
            backward = other * (1.0 - is_last)
            r_dual = -(dual_model - backward) - adjoint_field
            upward = r_dual + shifted(decay_field * r_dual, "tm", -1)
        else:
            stacked = jnp.stack([increment, dual_model]).reshape(2 * levels, row_count, col_count)
            applied = model_apply(
                with_halo(stacked, "space", 1, SUBSTEPS),
                jnp.concatenate([scaling_ext, scaling_ext]),
                jnp.concatenate([diff_coef, diff_coef]),
            )
            forward = shifted(applied[:levels], "tm", 1)
            backward = shifted(applied[levels:], "tm", -1)
            r_dual = -(dual_model - backward) - adjoint_field
            upward = r_dual + shifted(decay_field * r_dual, "tm", -1)

        obs_dual = obs_dual + (observed - obs_error * obs_dual - obs_image) / obs_error
        r_model = rhs_field - err_field * dual_model - (increment - forward)
        source = r_model - err_field * upward
        along = source
        along = source + decay_field * shifted(along, "tm", 1)
        dual_model = dual_model + upward
        increment = increment + along

        return (increment, dual_model, obs_dual)

    increment, dual_model, obs_dual = lax.fori_loop(
        0, ITERS, iteration, (increment, dual_model, obs_dual)
    )
    return (dual_model[None], obs_dual[None], increment[None])


def solution(mesh):
    in_specs = (
        P("tm", None, "space", None),
        P("tm", None, "space", None),
        P("tm", "space", None),
        P("tm", None, "space", None),
        P("tm", None, "space", None),
        P("tm", None, "space", None),
        P(None, "space", None),
        P(),
        P("tm", "space"),
        P("tm", "space", None),
        P("tm", "space", None, None),
        P("tm", "space", None),
        P("tm", "space", None),
    )
    out_specs = (P("tm", None, "space", None), P("tm", "space", None), P("tm", None, "space", None))
    return jax.shard_map(
        on_device, mesh=mesh, in_specs=in_specs, out_specs=out_specs, check_vma=False
    )
```

```python
import jax
import jax.numpy as jnp
from jax import lax
from jax.sharding import PartitionSpec as P

SUBSTEPS = 2
ITERS = 2
LANES = 128


def with_halo(cells, axis, dim, width):
    count = lax.axis_size(axis)
    ends = count - 1
    head = lax.slice_in_dim(cells, 0, width, axis=dim)
    tail = lax.slice_in_dim(cells, cells.shape[dim] - width, cells.shape[dim], axis=dim)
    return jnp.concatenate(
        [
            lax.ppermute(tail, axis, [(i, i + 1) for i in range(ends)]),
            cells,
            lax.ppermute(head, axis, [(i + 1, i) for i in range(ends)]),
        ],
        axis=dim,
    )


def shifted(value, axis, by):
    length = lax.axis_size(axis)
    pairs = [(i, i + by) for i in range(length) if 0 <= i + by < length]
    return lax.ppermute(value, axis, pairs)


def model_apply(current, scaling_ext, diff_coef):
    for step in range(SUBSTEPS):
        gain = scaling_ext[:, step : scaling_ext.shape[1] - step]
        scaled = gain * current
        inner = scaled[:, 1:-1]
        laplace = (
            scaled[:, 2:]
            + scaled[:, :-2]
            + jnp.roll(inner, 1, 2)
            + jnp.roll(inner, -1, 2)
            - 4.0 * inner
        )
        current = gain[:, 1:-1] * (inner + diff_coef * laplace)
    return current


def gather_cols(fields, row_oh, col_oh, group_mask):
    levels, row_count, col_count = fields.shape
    slots, lanes, touched = col_oh.shape
    groups = col_count // lanes
    lines = jnp.einsum(
        "sr,lrc->slc", row_oh, fields.astype(jnp.bfloat16), preferred_element_type=jnp.float32
    ).astype(jnp.bfloat16)
    lines = lines.reshape(slots, levels, groups, lanes)
    picked = jnp.einsum("slab,sbj->slaj", lines, col_oh, preferred_element_type=jnp.float32)
    picked = jnp.sum(picked * group_mask[:, None, :, :], axis=2)
    return picked.astype(jnp.bfloat16)


def spread_cols(values, row_oh, col_oh, group_mask, levels, col_count):
    slots, lanes, touched = col_oh.shape
    groups = col_count // lanes
    row_count = row_oh.shape[1]
    grads = values.reshape(slots, levels, 1, touched)
    placed = grads * group_mask[:, None, :, :].astype(jnp.bfloat16)
    lines = jnp.einsum("slaj,sbj->slab", placed, col_oh, preferred_element_type=jnp.float32)
    high = lax.reduce_precision(lines, exponent_bits=8, mantissa_bits=7)
    low = (lines - high).astype(jnp.bfloat16)
    high = high.astype(jnp.bfloat16)
    total = jnp.einsum(
        "sr,slab->lrab", row_oh, high, preferred_element_type=jnp.float32
    ) + jnp.einsum("sr,slab->lrab", row_oh, low, preferred_element_type=jnp.float32)
    return total.reshape(levels, row_count, groups * lanes)


def on_device(
    increment_start,
    dual_model_start,
    dual_obs_start,
    model_rhs,
    err_var,
    decays,
    scaling,
    diffusion,
    owners,
    tile_cols,
    jacobian,
    innovation,
    obs_var,
):
    increment = increment_start[0]
    dual_model = dual_model_start[0]
    rhs_field = model_rhs[0]
    err_field = err_var[0]
    decay_field = decays[0]
    owner_list = owners[0]
    cell_index = tile_cols[0]
    observed = innovation[0].astype(jnp.float32)
    obs_error = obs_var[0].astype(jnp.float32)
    obs_dual = dual_obs_start[0].astype(jnp.float32)
    levels, row_count, col_count = increment.shape
    tiles_here, orows, touch_levels = jacobian.shape[1:]
    touched = touch_levels // levels
    owners_count = lax.axis_size("space")
    tm_count = lax.axis_size("tm")
    tm_here = lax.axis_index("tm")
    capacity = max(2, 2 * tiles_here // owners_count)
    slots_all = owners_count * capacity
    groups = col_count // LANES
    diff_coef = diffusion[:, None, None]

    jac_tiles = jacobian[0]

    one_hot = (owner_list[:, None] == jnp.arange(owners_count, dtype=jnp.int32)[None, :]).astype(
        jnp.int32
    )
    earlier_count = jnp.cumsum(one_hot, axis=0) - one_hot
    slot_rank = jnp.sum(earlier_count * one_hot, axis=1)
    position = owner_list * capacity + slot_rank
    slot_oh = (position[:, None] == jnp.arange(slots_all, dtype=jnp.int32)[None, :]).astype(
        jnp.bfloat16
    )
    packed_cells = jnp.zeros((slots_all, touched), jnp.int32).at[position].set(cell_index)
    requests = lax.all_to_all(
        packed_cells.reshape(owners_count, capacity, touched),
        "space",
        split_axis=0,
        concat_axis=0,
        tiled=True,
    ).reshape(slots_all, touched)
    req_rows = requests[:, 0] // col_count
    req_cols = requests % col_count
    row_oh = (req_rows[:, None] == jnp.arange(row_count, dtype=jnp.int32)[None, :])
    col_oh = (
        (req_cols % LANES)[:, None, :] == jnp.arange(LANES, dtype=jnp.int32)[None, :, None]
    ).astype(jnp.bfloat16)
    group_mask = (
        (req_cols // LANES)[:, None, :] == jnp.arange(groups, dtype=jnp.int32)[None, :, None]
    ).astype(jnp.float32)

    scaling_ext = None
    is_first = (tm_here == 0).astype(jnp.float32)
    is_last = (tm_here == tm_count - 1).astype(jnp.float32)

    for repeat in range(ITERS):
        wanted = gather_cols(increment, row_oh.astype(jnp.bfloat16), col_oh, group_mask)
        tile_grad = jnp.einsum(
            "toj,to->tj", jac_tiles, obs_dual.astype(jnp.bfloat16), preferred_element_type=jnp.float32
        ).astype(jnp.bfloat16)
        sent_grad = jnp.einsum(
            "ts,tjl->slj",
            slot_oh,
            tile_grad.reshape(tiles_here, touched, levels),
            preferred_element_type=jnp.float32,
        ).astype(jnp.bfloat16)
        both = jnp.stack(
            [
                wanted.reshape(owners_count, capacity * levels, touched),
                sent_grad.reshape(owners_count, capacity * levels, touched),
            ],
            axis=1,
        )
        got = lax.all_to_all(both, "space", split_axis=0, concat_axis=0, tiled=True)
        got_cols = got[:, 0].reshape(slots_all, touch_levels)
        got_grad = got[:, 1].reshape(slots_all, touch_levels)
        own_cols = jnp.einsum(
            "ts,slj->tjl",
            slot_oh,
            got_cols.reshape(slots_all, levels, touched),
            preferred_element_type=jnp.float32,
        ).astype(jnp.bfloat16).reshape(tiles_here, touch_levels)
        obs_image = jnp.einsum(
            "toj,tj->to", jac_tiles, own_cols, preferred_element_type=jnp.float32
        )
        adjoint_field = spread_cols(
            got_grad, row_oh.astype(jnp.bfloat16), col_oh, group_mask, levels, col_count
        )

        if tm_count == 2:
            chosen = jnp.where(tm_here == 0, increment, dual_model)
            if scaling_ext is None:
                both_ext = with_halo(jnp.stack([scaling, chosen]), "space", 2, SUBSTEPS)
                scaling_ext, chosen_ext = both_ext[0], both_ext[1]
            else:
                chosen_ext = with_halo(chosen, "space", 1, SUBSTEPS)
            applied = model_apply(chosen_ext, scaling_ext, diff_coef)
            other = lax.ppermute(applied, "tm", [(0, 1), (1, 0)])
            forward = other * (1.0 - is_first)
            backward = other * (1.0 - is_last)
            r_dual = -(dual_model - backward) - adjoint_field
            upward = r_dual + shifted(decay_field * r_dual, "tm", -1)
        else:
            if scaling_ext is None:
                scaling_ext = with_halo(scaling, "space", 1, SUBSTEPS)
            stacked = jnp.stack([increment, dual_model]).reshape(2 * levels, row_count, col_count)
            applied = model_apply(
                with_halo(stacked, "space", 1, SUBSTEPS),
                jnp.concatenate([scaling_ext, scaling_ext]),
                jnp.concatenate([diff_coef, diff_coef]),
            )
            forward = shifted(applied[:levels], "tm", 1)
            backward = shifted(applied[levels:], "tm", -1)
            r_dual = -(dual_model - backward) - adjoint_field
            upward = r_dual + shifted(decay_field * r_dual, "tm", -1)

        obs_dual = obs_dual + (observed - obs_error * obs_dual - obs_image) / obs_error
        r_model = rhs_field - err_field * dual_model - (increment - forward)
        source = r_model - err_field * upward
        along = source
        along = source + decay_field * shifted(along, "tm", 1)
        dual_model = dual_model + upward
        increment = increment + along
    return (dual_model[None], obs_dual[None], increment[None])


def solution(mesh):
    in_specs = (
        P("tm", None, "space", None),
        P("tm", None, "space", None),
        P("tm", "space", None),
        P("tm", None, "space", None),
        P("tm", None, "space", None),
        P("tm", None, "space", None),
        P(None, "space", None),
        P(),
        P("tm", "space"),
        P("tm", "space", None),
        P("tm", "space", None, None),
        P("tm", "space", None),
        P("tm", "space", None),
    )
    out_specs = (P("tm", None, "space", None), P("tm", "space", None), P("tm", None, "space", None))
    return jax.shard_map(
        on_device, mesh=mesh, in_specs=in_specs, out_specs=out_specs, check_vma=False
    )
```

```python
import jax
import jax.numpy as jnp
from jax import lax
from jax.sharding import PartitionSpec as P

SUBSTEPS = 2
ITERS = 2
LANES = 128


def with_halo(cells, axis, dim, width):
    count = lax.axis_size(axis)
    ends = count - 1
    head = lax.slice_in_dim(cells, 0, width, axis=dim)
    tail = lax.slice_in_dim(cells, cells.shape[dim] - width, cells.shape[dim], axis=dim)
    return jnp.concatenate(
        [
            lax.ppermute(tail, axis, [(i, i + 1) for i in range(ends)]),
            cells,
            lax.ppermute(head, axis, [(i + 1, i) for i in range(ends)]),
        ],
        axis=dim,
    )


def shifted(value, axis, by):
    length = lax.axis_size(axis)
    pairs = [(i, i + by) for i in range(length) if 0 <= i + by < length]
    return lax.ppermute(value, axis, pairs)


def model_apply(current, scaling_ext, diff_coef):
    for step in range(SUBSTEPS):
        gain = scaling_ext[:, step : scaling_ext.shape[1] - step]
        scaled = gain * current
        inner = scaled[:, 1:-1]
        laplace = (
            scaled[:, 2:]
            + scaled[:, :-2]
            + jnp.roll(inner, 1, 2)
            + jnp.roll(inner, -1, 2)
            - 4.0 * inner
        )
        current = gain[:, 1:-1] * (inner + diff_coef * laplace)
    return current


def gather_cols(fields, row_oh, col_oh, group_mask):
    levels, row_count, col_count = fields.shape
    slots, lanes, touched = col_oh.shape
    groups = col_count // lanes
    lines = jnp.einsum(
        "sr,lrc->slc", row_oh, fields.astype(jnp.bfloat16), preferred_element_type=jnp.float32
    ).astype(jnp.bfloat16)
    lines = lines.reshape(slots, levels, groups, lanes)
    picked = jnp.einsum("slab,sbj->slaj", lines, col_oh, preferred_element_type=jnp.float32)
    picked = jnp.sum(picked * group_mask[:, None, :, :], axis=2)
    return picked.astype(jnp.bfloat16)


def spread_cols(values, row_oh, col_oh, group_mask, levels, col_count):
    slots, lanes, touched = col_oh.shape
    groups = col_count // lanes
    row_count = row_oh.shape[1]
    grads = values.reshape(slots, levels, 1, touched)
    placed = grads * group_mask[:, None, :, :].astype(jnp.bfloat16)
    lines = jnp.einsum("slaj,sbj->slab", placed, col_oh, preferred_element_type=jnp.float32)
    high = lax.reduce_precision(lines, exponent_bits=8, mantissa_bits=7)
    low = (lines - high).astype(jnp.bfloat16)
    high = high.astype(jnp.bfloat16)
    total = jnp.einsum(
        "sr,slab->lrab", row_oh, high, preferred_element_type=jnp.float32
    ) + jnp.einsum("sr,slab->lrab", row_oh, low, preferred_element_type=jnp.float32)
    return total.reshape(levels, row_count, groups * lanes)


def on_device(
    increment_start,
    dual_model_start,
    dual_obs_start,
    model_rhs,
    err_var,
    decays,
    scaling,
    diffusion,
    owners,
    tile_cols,
    jacobian,
    innovation,
    obs_var,
):
    increment = increment_start[0]
    dual_model = dual_model_start[0]
    rhs_field = model_rhs[0]
    err_field = err_var[0]
    decay_field = decays[0]
    owner_list = owners[0]
    cell_index = tile_cols[0]
    observed = innovation[0].astype(jnp.float32)
    obs_error = obs_var[0].astype(jnp.float32)
    obs_dual = dual_obs_start[0].astype(jnp.float32)
    levels, row_count, col_count = increment.shape
    tiles_here, orows, touch_levels = jacobian.shape[1:]
    touched = touch_levels // levels
    owners_count = lax.axis_size("space")
    tm_count = lax.axis_size("tm")
    tm_here = lax.axis_index("tm")
    capacity = max(2, 2 * tiles_here // owners_count)
    slots_all = owners_count * capacity
    groups = col_count // LANES
    diff_coef = diffusion[:, None, None]

    jac_tiles = jacobian[0]

    one_hot = (owner_list[:, None] == jnp.arange(owners_count, dtype=jnp.int32)[None, :]).astype(
        jnp.int32
    )
    earlier_count = jnp.cumsum(one_hot, axis=0) - one_hot
    slot_rank = jnp.sum(earlier_count * one_hot, axis=1)
    position = owner_list * capacity + slot_rank
    slot_oh = (position[:, None] == jnp.arange(slots_all, dtype=jnp.int32)[None, :]).astype(
        jnp.bfloat16
    )
    packed_cells = jnp.zeros((slots_all, touched), jnp.int32).at[position].set(cell_index)
    requests = lax.all_to_all(
        packed_cells.reshape(owners_count, capacity, touched),
        "space",
        split_axis=0,
        concat_axis=0,
        tiled=True,
    ).reshape(slots_all, touched)
    req_rows = requests[:, 0] // col_count
    req_cols = requests % col_count
    row_oh = (req_rows[:, None] == jnp.arange(row_count, dtype=jnp.int32)[None, :])
    col_oh = (
        (req_cols % LANES)[:, None, :] == jnp.arange(LANES, dtype=jnp.int32)[None, :, None]
    ).astype(jnp.bfloat16)
    group_mask = (
        (req_cols // LANES)[:, None, :] == jnp.arange(groups, dtype=jnp.int32)[None, :, None]
    ).astype(jnp.float32)

    scaling_ext = None
    is_first = (tm_here == 0).astype(jnp.float32)
    is_last = (tm_here == tm_count - 1).astype(jnp.float32)

    for repeat in range(ITERS):
        wanted = gather_cols(increment, row_oh.astype(jnp.bfloat16), col_oh, group_mask)
        tile_grad = jnp.einsum(
            "toj,to->tj", jac_tiles, obs_dual.astype(jnp.bfloat16), preferred_element_type=jnp.float32
        ).astype(jnp.bfloat16)
        sent_grad = jnp.einsum(
            "ts,tjl->slj",
            slot_oh,
            tile_grad.reshape(tiles_here, touched, levels),
            preferred_element_type=jnp.float32,
        ).astype(jnp.bfloat16)
        both = jnp.stack(
            [
                wanted.reshape(owners_count, capacity * levels, touched),
                sent_grad.reshape(owners_count, capacity * levels, touched),
            ],
            axis=1,
        )
        if tm_count == 2:
            chosen = jnp.where(tm_here == 0, increment, dual_model)
            if scaling_ext is None:
                both_ext = with_halo(jnp.stack([scaling, chosen]), "space", 2, SUBSTEPS)
                scaling_ext, chosen_ext = both_ext[0], both_ext[1]
            else:
                chosen_ext = with_halo(chosen, "space", 1, SUBSTEPS)
            both, chosen_ext = lax.optimization_barrier((both, chosen_ext))
        got = lax.all_to_all(both, "space", split_axis=0, concat_axis=0, tiled=True)
        got_cols = got[:, 0].reshape(slots_all, touch_levels)
        got_grad = got[:, 1].reshape(slots_all, touch_levels)
        own_cols = jnp.einsum(
            "ts,slj->tjl",
            slot_oh,
            got_cols.reshape(slots_all, levels, touched),
            preferred_element_type=jnp.float32,
        ).astype(jnp.bfloat16).reshape(tiles_here, touch_levels)
        obs_image = jnp.einsum(
            "toj,tj->to", jac_tiles, own_cols, preferred_element_type=jnp.float32
        )
        adjoint_field = spread_cols(
            got_grad, row_oh.astype(jnp.bfloat16), col_oh, group_mask, levels, col_count
        )

        if tm_count == 2:
            applied = model_apply(chosen_ext, scaling_ext, diff_coef)
            other = lax.ppermute(applied, "tm", [(0, 1), (1, 0)])
            forward = other * (1.0 - is_first)
            backward = other * (1.0 - is_last)
            r_dual = -(dual_model - backward) - adjoint_field
            upward = r_dual + shifted(decay_field * r_dual, "tm", -1)
        else:
            if scaling_ext is None:
                scaling_ext = with_halo(scaling, "space", 1, SUBSTEPS)
            stacked = jnp.stack([increment, dual_model]).reshape(2 * levels, row_count, col_count)
            applied = model_apply(
                with_halo(stacked, "space", 1, SUBSTEPS),
                jnp.concatenate([scaling_ext, scaling_ext]),
                jnp.concatenate([diff_coef, diff_coef]),
            )
            forward = shifted(applied[:levels], "tm", 1)
            backward = shifted(applied[levels:], "tm", -1)
            r_dual = -(dual_model - backward) - adjoint_field
            upward = r_dual + shifted(decay_field * r_dual, "tm", -1)

        obs_dual = obs_dual + (observed - obs_error * obs_dual - obs_image) / obs_error
        r_model = rhs_field - err_field * dual_model - (increment - forward)
        source = r_model - err_field * upward
        along = source
        along = source + decay_field * shifted(along, "tm", 1)
        dual_model = dual_model + upward
        increment = increment + along
    return (dual_model[None], obs_dual[None], increment[None])


def solution(mesh):
    in_specs = (
        P("tm", None, "space", None),
        P("tm", None, "space", None),
        P("tm", "space", None),
        P("tm", None, "space", None),
        P("tm", None, "space", None),
        P("tm", None, "space", None),
        P(None, "space", None),
        P(),
        P("tm", "space"),
        P("tm", "space", None),
        P("tm", "space", None, None),
        P("tm", "space", None),
        P("tm", "space", None),
    )
    out_specs = (P("tm", None, "space", None), P("tm", "space", None), P("tm", None, "space", None))
    return jax.shard_map(
        on_device, mesh=mesh, in_specs=in_specs, out_specs=out_specs, check_vma=False
    )
```

```python
import jax
import jax.numpy as jnp
from jax import lax
from jax.sharding import PartitionSpec as P

SUBSTEPS = 2
ITERS = 2
LANES = 128


def with_halo(cells, axis, dim, width):
    count = lax.axis_size(axis)
    ends = count - 1
    head = lax.slice_in_dim(cells, 0, width, axis=dim)
    tail = lax.slice_in_dim(cells, cells.shape[dim] - width, cells.shape[dim], axis=dim)
    return jnp.concatenate(
        [
            lax.ppermute(tail, axis, [(i, i + 1) for i in range(ends)]),
            cells,
            lax.ppermute(head, axis, [(i + 1, i) for i in range(ends)]),
        ],
        axis=dim,
    )


def shifted(value, axis, by):
    length = lax.axis_size(axis)
    pairs = [(i, i + by) for i in range(length) if 0 <= i + by < length]
    return lax.ppermute(value, axis, pairs)


def model_apply(current, scaling_ext, diff_coef):
    for step in range(SUBSTEPS):
        gain = scaling_ext[:, step : scaling_ext.shape[1] - step]
        scaled = gain * current
        inner = scaled[:, 1:-1]
        laplace = (
            scaled[:, 2:]
            + scaled[:, :-2]
            + jnp.roll(inner, 1, 2)
            + jnp.roll(inner, -1, 2)
            - 4.0 * inner
        )
        current = gain[:, 1:-1] * (inner + diff_coef * laplace)
    return current


def gather_cols(fields, row_oh, col_oh, group_mask):
    levels, row_count, col_count = fields.shape
    slots, lanes, touched = col_oh.shape
    groups = col_count // lanes
    lines = jnp.einsum(
        "sr,lrc->slc", row_oh, fields.astype(jnp.bfloat16), preferred_element_type=jnp.float32
    ).astype(jnp.bfloat16)
    lines = lines.reshape(slots, levels, groups, lanes)
    picked = jnp.einsum("slab,sbj->slaj", lines, col_oh, preferred_element_type=jnp.float32)
    picked = jnp.sum(picked * group_mask[:, None, :, :], axis=2)
    return picked.astype(jnp.bfloat16)


def spread_cols(values, row_oh, col_oh, group_mask, levels, col_count):
    slots, lanes, touched = col_oh.shape
    groups = col_count // lanes
    row_count = row_oh.shape[1]
    grads = values.reshape(slots, levels, 1, touched)
    placed = grads * group_mask[:, None, :, :].astype(jnp.bfloat16)
    lines = jnp.einsum("slaj,sbj->slab", placed, col_oh, preferred_element_type=jnp.float32)
    total = jnp.einsum(
        "sr,slab->lrab", row_oh, lines.astype(jnp.bfloat16), preferred_element_type=jnp.float32
    )
    return total.reshape(levels, row_count, groups * lanes)


def on_device(
    increment_start,
    dual_model_start,
    dual_obs_start,
    model_rhs,
    err_var,
    decays,
    scaling,
    diffusion,
    owners,
    tile_cols,
    jacobian,
    innovation,
    obs_var,
):
    increment = increment_start[0]
    dual_model = dual_model_start[0]
    rhs_field = model_rhs[0]
    err_field = err_var[0]
    decay_field = decays[0]
    owner_list = owners[0]
    cell_index = tile_cols[0]
    observed = innovation[0].astype(jnp.float32)
    obs_error = obs_var[0].astype(jnp.float32)
    obs_dual = dual_obs_start[0].astype(jnp.float32)
    levels, row_count, col_count = increment.shape
    tiles_here, orows, touch_levels = jacobian.shape[1:]
    touched = touch_levels // levels
    owners_count = lax.axis_size("space")
    tm_count = lax.axis_size("tm")
    tm_here = lax.axis_index("tm")
    capacity = max(2, 2 * tiles_here // owners_count)
    slots_all = owners_count * capacity
    groups = col_count // LANES
    diff_coef = diffusion[:, None, None]

    jac_tiles = jacobian[0]

    one_hot = (owner_list[:, None] == jnp.arange(owners_count, dtype=jnp.int32)[None, :]).astype(
        jnp.int32
    )
    earlier_count = jnp.cumsum(one_hot, axis=0) - one_hot
    slot_rank = jnp.sum(earlier_count * one_hot, axis=1)
    position = owner_list * capacity + slot_rank
    slot_oh = (position[:, None] == jnp.arange(slots_all, dtype=jnp.int32)[None, :]).astype(
        jnp.bfloat16
    )
    packed_cells = jnp.zeros((slots_all, touched), jnp.int32).at[position].set(cell_index)
    requests = lax.all_to_all(
        packed_cells.reshape(owners_count, capacity, touched),
        "space",
        split_axis=0,
        concat_axis=0,
        tiled=True,
    ).reshape(slots_all, touched)
    req_rows = requests[:, 0] // col_count
    req_cols = requests % col_count
    row_oh = (req_rows[:, None] == jnp.arange(row_count, dtype=jnp.int32)[None, :])
    col_oh = (
        (req_cols % LANES)[:, None, :] == jnp.arange(LANES, dtype=jnp.int32)[None, :, None]
    ).astype(jnp.bfloat16)
    group_mask = (
        (req_cols // LANES)[:, None, :] == jnp.arange(groups, dtype=jnp.int32)[None, :, None]
    ).astype(jnp.float32)

    scaling_ext = None
    is_first = (tm_here == 0).astype(jnp.float32)
    is_last = (tm_here == tm_count - 1).astype(jnp.float32)

    for repeat in range(ITERS):
        wanted = gather_cols(increment, row_oh.astype(jnp.bfloat16), col_oh, group_mask)
        tile_grad = jnp.einsum(
            "toj,to->tj", jac_tiles, obs_dual.astype(jnp.bfloat16), preferred_element_type=jnp.float32
        ).astype(jnp.bfloat16)
        sent_grad = jnp.einsum(
            "ts,tjl->slj",
            slot_oh,
            tile_grad.reshape(tiles_here, touched, levels),
            preferred_element_type=jnp.float32,
        ).astype(jnp.bfloat16)
        both = jnp.stack(
            [
                wanted.reshape(owners_count, capacity * levels, touched),
                sent_grad.reshape(owners_count, capacity * levels, touched),
            ],
            axis=1,
        )
        got = lax.all_to_all(both, "space", split_axis=0, concat_axis=0, tiled=True)
        got_cols = got[:, 0].reshape(slots_all, touch_levels)
        got_grad = got[:, 1].reshape(slots_all, touch_levels)
        own_cols = jnp.einsum(
            "ts,slj->tjl",
            slot_oh,
            got_cols.reshape(slots_all, levels, touched),
            preferred_element_type=jnp.float32,
        ).astype(jnp.bfloat16).reshape(tiles_here, touch_levels)
        obs_image = jnp.einsum(
            "toj,tj->to", jac_tiles, own_cols, preferred_element_type=jnp.float32
        )
        adjoint_field = spread_cols(
            got_grad, row_oh.astype(jnp.bfloat16), col_oh, group_mask, levels, col_count
        )

        if tm_count == 2:
            chosen = jnp.where(tm_here == 0, increment, dual_model)
            if scaling_ext is None:
                both_ext = with_halo(jnp.stack([scaling, chosen]), "space", 2, SUBSTEPS)
                scaling_ext, chosen_ext = both_ext[0], both_ext[1]
            else:
                chosen_ext = with_halo(chosen, "space", 1, SUBSTEPS)
            applied = model_apply(chosen_ext, scaling_ext, diff_coef)
            other = lax.ppermute(applied, "tm", [(0, 1), (1, 0)])
            forward = other * (1.0 - is_first)
            backward = other * (1.0 - is_last)
            r_dual = -(dual_model - backward) - adjoint_field
            upward = r_dual + shifted(decay_field * r_dual, "tm", -1)
        else:
            if scaling_ext is None:
                scaling_ext = with_halo(scaling, "space", 1, SUBSTEPS)
            stacked = jnp.stack([increment, dual_model]).reshape(2 * levels, row_count, col_count)
            applied = model_apply(
                with_halo(stacked, "space", 1, SUBSTEPS),
                jnp.concatenate([scaling_ext, scaling_ext]),
                jnp.concatenate([diff_coef, diff_coef]),
            )
            forward = shifted(applied[:levels], "tm", 1)
            backward = shifted(applied[levels:], "tm", -1)
            r_dual = -(dual_model - backward) - adjoint_field
            upward = r_dual + shifted(decay_field * r_dual, "tm", -1)

        obs_dual = obs_dual + (observed - obs_error * obs_dual - obs_image) / obs_error
        r_model = rhs_field - err_field * dual_model - (increment - forward)
        source = r_model - err_field * upward
        along = source
        along = source + decay_field * shifted(along, "tm", 1)
        dual_model = dual_model + upward
        increment = increment + along
    return (dual_model[None], obs_dual[None], increment[None])


def solution(mesh):
    in_specs = (
        P("tm", None, "space", None),
        P("tm", None, "space", None),
        P("tm", "space", None),
        P("tm", None, "space", None),
        P("tm", None, "space", None),
        P("tm", None, "space", None),
        P(None, "space", None),
        P(),
        P("tm", "space"),
        P("tm", "space", None),
        P("tm", "space", None, None),
        P("tm", "space", None),
        P("tm", "space", None),
    )
    out_specs = (P("tm", None, "space", None), P("tm", "space", None), P("tm", None, "space", None))
    return jax.shard_map(
        on_device, mesh=mesh, in_specs=in_specs, out_specs=out_specs, check_vma=False
    )
```

```python
import jax
import jax.numpy as jnp
from jax import lax
from jax.sharding import PartitionSpec as P

SUBSTEPS = 2
ITERS = 2
LANES = 128


def with_halo(cells, axis, dim, width):
    count = lax.axis_size(axis)
    ends = count - 1
    head = lax.slice_in_dim(cells, 0, width, axis=dim)
    tail = lax.slice_in_dim(cells, cells.shape[dim] - width, cells.shape[dim], axis=dim)
    return jnp.concatenate(
        [
            lax.ppermute(tail, axis, [(i, i + 1) for i in range(ends)]),
            cells,
            lax.ppermute(head, axis, [(i + 1, i) for i in range(ends)]),
        ],
        axis=dim,
    )


def shifted(value, axis, by):
    length = lax.axis_size(axis)
    pairs = [(i, i + by) for i in range(length) if 0 <= i + by < length]
    return lax.ppermute(value, axis, pairs)


def model_apply(current, scaling_ext, diff_coef):
    for step in range(SUBSTEPS):
        gain = scaling_ext[:, step : scaling_ext.shape[1] - step]
        scaled = gain * current
        inner = scaled[:, 1:-1]
        laplace = (
            scaled[:, 2:]
            + scaled[:, :-2]
            + jnp.roll(inner, 1, 2)
            + jnp.roll(inner, -1, 2)
            - 4.0 * inner
        )
        current = gain[:, 1:-1] * (inner + diff_coef * laplace)
    return current


def gather_cols(fields, row_oh, col_oh, group_mask):
    levels, row_count, col_count = fields.shape
    slots, lanes, touched = col_oh.shape
    groups = col_count // lanes
    lines = jnp.einsum(
        "sr,lrc->slc", row_oh, fields.astype(jnp.bfloat16), preferred_element_type=jnp.float32
    ).astype(jnp.bfloat16)
    lines = lines.reshape(slots, levels, groups, lanes)
    picked = jnp.einsum("slab,sbj->slaj", lines, col_oh, preferred_element_type=jnp.float32)
    picked = jnp.sum(picked * group_mask[:, None, :, :], axis=2)
    return picked.astype(jnp.bfloat16)


def spread_cols(values, row_oh, col_oh, group_mask, levels, col_count):
    slots, lanes, touched = col_oh.shape
    groups = col_count // lanes
    row_count = row_oh.shape[1]
    grads = values.reshape(slots, levels, 1, touched)
    placed = grads * group_mask[:, None, :, :].astype(jnp.bfloat16)
    lines = jnp.einsum("slaj,sbj->slab", placed, col_oh, preferred_element_type=jnp.float32)
    total = jnp.einsum(
        "sr,slab->lrab", row_oh, lines.astype(jnp.bfloat16), preferred_element_type=jnp.float32
    )
    return lax.optimization_barrier(total.reshape(levels, row_count, groups * lanes))


def on_device(
    increment_start,
    dual_model_start,
    dual_obs_start,
    model_rhs,
    err_var,
    decays,
    scaling,
    diffusion,
    owners,
    tile_cols,
    jacobian,
    innovation,
    obs_var,
):
    increment = increment_start[0]
    dual_model = dual_model_start[0]
    rhs_field = model_rhs[0]
    err_field = err_var[0]
    decay_field = decays[0]
    owner_list = owners[0]
    cell_index = tile_cols[0]
    observed = innovation[0].astype(jnp.float32)
    obs_error = obs_var[0].astype(jnp.float32)
    obs_dual = dual_obs_start[0].astype(jnp.float32)
    levels, row_count, col_count = increment.shape
    tiles_here, orows, touch_levels = jacobian.shape[1:]
    touched = touch_levels // levels
    owners_count = lax.axis_size("space")
    tm_count = lax.axis_size("tm")
    tm_here = lax.axis_index("tm")
    capacity = max(2, 2 * tiles_here // owners_count)
    slots_all = owners_count * capacity
    groups = col_count // LANES
    diff_coef = diffusion[:, None, None]

    jac_tiles = jacobian[0]

    one_hot = (owner_list[:, None] == jnp.arange(owners_count, dtype=jnp.int32)[None, :]).astype(
        jnp.int32
    )
    earlier_count = jnp.cumsum(one_hot, axis=0) - one_hot
    slot_rank = jnp.sum(earlier_count * one_hot, axis=1)
    position = owner_list * capacity + slot_rank
    slot_oh = (position[:, None] == jnp.arange(slots_all, dtype=jnp.int32)[None, :]).astype(
        jnp.bfloat16
    )
    packed_cells = jnp.zeros((slots_all, touched), jnp.int32).at[position].set(cell_index)
    requests = lax.all_to_all(
        packed_cells.reshape(owners_count, capacity, touched),
        "space",
        split_axis=0,
        concat_axis=0,
        tiled=True,
    ).reshape(slots_all, touched)
    req_rows = requests[:, 0] // col_count
    req_cols = requests % col_count
    row_oh = (req_rows[:, None] == jnp.arange(row_count, dtype=jnp.int32)[None, :])
    col_oh = (
        (req_cols % LANES)[:, None, :] == jnp.arange(LANES, dtype=jnp.int32)[None, :, None]
    ).astype(jnp.bfloat16)
    group_mask = (
        (req_cols // LANES)[:, None, :] == jnp.arange(groups, dtype=jnp.int32)[None, :, None]
    ).astype(jnp.float32)

    scaling_ext = None
    is_first = (tm_here == 0).astype(jnp.float32)
    is_last = (tm_here == tm_count - 1).astype(jnp.float32)

    for repeat in range(ITERS):
        wanted = gather_cols(increment, row_oh.astype(jnp.bfloat16), col_oh, group_mask)
        tile_grad = jnp.einsum(
            "toj,to->tj", jac_tiles, obs_dual.astype(jnp.bfloat16), preferred_element_type=jnp.float32
        ).astype(jnp.bfloat16)
        sent_grad = jnp.einsum(
            "ts,tjl->slj",
            slot_oh,
            tile_grad.reshape(tiles_here, touched, levels),
            preferred_element_type=jnp.float32,
        ).astype(jnp.bfloat16)
        both = jnp.stack(
            [
                wanted.reshape(owners_count, capacity * levels, touched),
                sent_grad.reshape(owners_count, capacity * levels, touched),
            ],
            axis=1,
        )
        got = lax.all_to_all(both, "space", split_axis=0, concat_axis=0, tiled=True)
        got_cols = got[:, 0].reshape(slots_all, touch_levels)
        got_grad = got[:, 1].reshape(slots_all, touch_levels)
        own_cols = jnp.einsum(
            "ts,slj->tjl",
            slot_oh,
            got_cols.reshape(slots_all, levels, touched),
            preferred_element_type=jnp.float32,
        ).astype(jnp.bfloat16).reshape(tiles_here, touch_levels)
        obs_image = jnp.einsum(
            "toj,tj->to", jac_tiles, own_cols, preferred_element_type=jnp.float32
        )
        adjoint_field = spread_cols(
            got_grad, row_oh.astype(jnp.bfloat16), col_oh, group_mask, levels, col_count
        )

        if tm_count == 2:
            chosen = jnp.where(tm_here == 0, increment, dual_model)
            if scaling_ext is None:
                both_ext = with_halo(jnp.stack([scaling, chosen]), "space", 2, SUBSTEPS)
                scaling_ext, chosen_ext = both_ext[0], both_ext[1]
            else:
                chosen_ext = with_halo(chosen, "space", 1, SUBSTEPS)
            applied = model_apply(chosen_ext, scaling_ext, diff_coef)
            other = lax.ppermute(applied, "tm", [(0, 1), (1, 0)])
            forward = other * (1.0 - is_first)
            backward = other * (1.0 - is_last)
            r_dual = -(dual_model - backward) - adjoint_field
            upward = r_dual + shifted(decay_field * r_dual, "tm", -1)
        else:
            if scaling_ext is None:
                scaling_ext = with_halo(scaling, "space", 1, SUBSTEPS)
            stacked = jnp.stack([increment, dual_model]).reshape(2 * levels, row_count, col_count)
            applied = model_apply(
                with_halo(stacked, "space", 1, SUBSTEPS),
                jnp.concatenate([scaling_ext, scaling_ext]),
                jnp.concatenate([diff_coef, diff_coef]),
            )
            forward = shifted(applied[:levels], "tm", 1)
            backward = shifted(applied[levels:], "tm", -1)
            r_dual = -(dual_model - backward) - adjoint_field
            upward = r_dual + shifted(decay_field * r_dual, "tm", -1)

        obs_dual = obs_dual + (observed - obs_error * obs_dual - obs_image) / obs_error
        r_model = rhs_field - err_field * dual_model - (increment - forward)
        source = r_model - err_field * upward
        along = source
        along = source + decay_field * shifted(along, "tm", 1)
        dual_model = dual_model + upward
        increment = increment + along
    return (dual_model[None], obs_dual[None], increment[None])


def solution(mesh):
    in_specs = (
        P("tm", None, "space", None),
        P("tm", None, "space", None),
        P("tm", "space", None),
        P("tm", None, "space", None),
        P("tm", None, "space", None),
        P("tm", None, "space", None),
        P(None, "space", None),
        P(),
        P("tm", "space"),
        P("tm", "space", None),
        P("tm", "space", None, None),
        P("tm", "space", None),
        P("tm", "space", None),
    )
    out_specs = (P("tm", None, "space", None), P("tm", "space", None), P("tm", None, "space", None))
    return jax.shard_map(
        on_device, mesh=mesh, in_specs=in_specs, out_specs=out_specs, check_vma=False
    )
```

```python
import jax
import jax.numpy as jnp
from jax import lax
from jax.sharding import PartitionSpec as P

SUBSTEPS = 2
ITERS = 2
LANES = 128


def with_halo(cells, axis, dim, width):
    count = lax.axis_size(axis)
    ends = count - 1
    head = lax.slice_in_dim(cells, 0, width, axis=dim)
    tail = lax.slice_in_dim(cells, cells.shape[dim] - width, cells.shape[dim], axis=dim)
    return jnp.concatenate(
        [
            lax.ppermute(tail, axis, [(i, i + 1) for i in range(ends)]),
            cells,
            lax.ppermute(head, axis, [(i + 1, i) for i in range(ends)]),
        ],
        axis=dim,
    )


def shifted(value, axis, by):
    length = lax.axis_size(axis)
    pairs = [(i, i + by) for i in range(length) if 0 <= i + by < length]
    return lax.ppermute(value, axis, pairs)


def model_apply(current, scaling_ext, diff_coef):
    for step in range(SUBSTEPS):
        gain = scaling_ext[:, step : scaling_ext.shape[1] - step]
        scaled = gain * current
        inner = scaled[:, 1:-1]
        laplace = (
            scaled[:, 2:]
            + scaled[:, :-2]
            + jnp.roll(inner, 1, 2)
            + jnp.roll(inner, -1, 2)
            - 4.0 * inner
        )
        current = gain[:, 1:-1] * (inner + diff_coef * laplace)
    return current


def gather_cols(fields, row_oh, col_oh, group_mask):
    levels, row_count, col_count = fields.shape
    slots, lanes, touched = col_oh.shape
    groups = col_count // lanes
    lines = jnp.einsum(
        "sr,lrc->slc", row_oh, fields.astype(jnp.bfloat16), preferred_element_type=jnp.float32
    ).astype(jnp.bfloat16)
    lines = lines.reshape(slots, levels, groups, lanes)
    picked = jnp.einsum("slab,sbj->slaj", lines, col_oh, preferred_element_type=jnp.float32)
    picked = jnp.sum(picked * group_mask[:, None, :, :], axis=2)
    return picked.astype(jnp.bfloat16)


def spread_cols(values, row_oh, col_oh, group_mask, levels, col_count):
    slots, lanes, touched = col_oh.shape
    groups = col_count // lanes
    row_count = row_oh.shape[1]
    grads = values.reshape(slots, 1, levels, touched)
    placed = grads * group_mask[:, :, None, :].astype(jnp.bfloat16)
    lines = jnp.einsum("salj,sbj->salb", placed, col_oh, preferred_element_type=jnp.float32)
    lines = lines.astype(jnp.bfloat16)
    parts = [
        jnp.einsum("sr,slb->lrb", row_oh, lines[:, a], preferred_element_type=jnp.float32)
        for a in range(groups)
    ]
    return jnp.concatenate(parts, axis=2)


def on_device(
    increment_start,
    dual_model_start,
    dual_obs_start,
    model_rhs,
    err_var,
    decays,
    scaling,
    diffusion,
    owners,
    tile_cols,
    jacobian,
    innovation,
    obs_var,
):
    increment = increment_start[0]
    dual_model = dual_model_start[0]
    rhs_field = model_rhs[0]
    err_field = err_var[0]
    decay_field = decays[0]
    owner_list = owners[0]
    cell_index = tile_cols[0]
    observed = innovation[0].astype(jnp.float32)
    obs_error = obs_var[0].astype(jnp.float32)
    obs_dual = dual_obs_start[0].astype(jnp.float32)
    levels, row_count, col_count = increment.shape
    tiles_here, orows, touch_levels = jacobian.shape[1:]
    touched = touch_levels // levels
    owners_count = lax.axis_size("space")
    tm_count = lax.axis_size("tm")
    tm_here = lax.axis_index("tm")
    capacity = max(2, 2 * tiles_here // owners_count)
    slots_all = owners_count * capacity
    groups = col_count // LANES
    diff_coef = diffusion[:, None, None]

    jac_tiles = jacobian[0]

    one_hot = (owner_list[:, None] == jnp.arange(owners_count, dtype=jnp.int32)[None, :]).astype(
        jnp.int32
    )
    earlier_count = jnp.cumsum(one_hot, axis=0) - one_hot
    slot_rank = jnp.sum(earlier_count * one_hot, axis=1)
    position = owner_list * capacity + slot_rank
    slot_oh = (position[:, None] == jnp.arange(slots_all, dtype=jnp.int32)[None, :]).astype(
        jnp.bfloat16
    )
    packed_cells = jnp.zeros((slots_all, touched), jnp.int32).at[position].set(cell_index)
    requests = lax.all_to_all(
        packed_cells.reshape(owners_count, capacity, touched),
        "space",
        split_axis=0,
        concat_axis=0,
        tiled=True,
    ).reshape(slots_all, touched)
    req_rows = requests[:, 0] // col_count
    req_cols = requests % col_count
    row_oh = (req_rows[:, None] == jnp.arange(row_count, dtype=jnp.int32)[None, :])
    col_oh = (
        (req_cols % LANES)[:, None, :] == jnp.arange(LANES, dtype=jnp.int32)[None, :, None]
    ).astype(jnp.bfloat16)
    group_mask = (
        (req_cols // LANES)[:, None, :] == jnp.arange(groups, dtype=jnp.int32)[None, :, None]
    ).astype(jnp.float32)

    scaling_ext = None
    is_first = (tm_here == 0).astype(jnp.float32)
    is_last = (tm_here == tm_count - 1).astype(jnp.float32)

    for repeat in range(ITERS):
        wanted = gather_cols(increment, row_oh.astype(jnp.bfloat16), col_oh, group_mask)
        tile_grad = jnp.einsum(
            "toj,to->tj", jac_tiles, obs_dual.astype(jnp.bfloat16), preferred_element_type=jnp.float32
        ).astype(jnp.bfloat16)
        sent_grad = jnp.einsum(
            "ts,tjl->slj",
            slot_oh,
            tile_grad.reshape(tiles_here, touched, levels),
            preferred_element_type=jnp.float32,
        ).astype(jnp.bfloat16)
        both = jnp.stack(
            [
                wanted.reshape(owners_count, capacity * levels, touched),
                sent_grad.reshape(owners_count, capacity * levels, touched),
            ],
            axis=1,
        )
        got = lax.all_to_all(both, "space", split_axis=0, concat_axis=0, tiled=True)
        got_cols = got[:, 0].reshape(slots_all, touch_levels)
        got_grad = got[:, 1].reshape(slots_all, touch_levels)
        own_cols = jnp.einsum(
            "ts,slj->tjl",
            slot_oh,
            got_cols.reshape(slots_all, levels, touched),
            preferred_element_type=jnp.float32,
        ).astype(jnp.bfloat16).reshape(tiles_here, touch_levels)
        obs_image = jnp.einsum(
            "toj,tj->to", jac_tiles, own_cols, preferred_element_type=jnp.float32
        )
        adjoint_field = spread_cols(
            got_grad, row_oh.astype(jnp.bfloat16), col_oh, group_mask, levels, col_count
        )

        if tm_count == 2:
            chosen = jnp.where(tm_here == 0, increment, dual_model)
            if scaling_ext is None:
                both_ext = with_halo(jnp.stack([scaling, chosen]), "space", 2, SUBSTEPS)
                scaling_ext, chosen_ext = both_ext[0], both_ext[1]
            else:
                chosen_ext = with_halo(chosen, "space", 1, SUBSTEPS)
            applied = model_apply(chosen_ext, scaling_ext, diff_coef)
            other = lax.ppermute(applied, "tm", [(0, 1), (1, 0)])
            forward = other * (1.0 - is_first)
            backward = other * (1.0 - is_last)
            r_dual = -(dual_model - backward) - adjoint_field
            upward = r_dual + shifted(decay_field * r_dual, "tm", -1)
        else:
            if scaling_ext is None:
                scaling_ext = with_halo(scaling, "space", 1, SUBSTEPS)
            stacked = jnp.stack([increment, dual_model]).reshape(2 * levels, row_count, col_count)
            applied = model_apply(
                with_halo(stacked, "space", 1, SUBSTEPS),
                jnp.concatenate([scaling_ext, scaling_ext]),
                jnp.concatenate([diff_coef, diff_coef]),
            )
            forward = shifted(applied[:levels], "tm", 1)
            backward = shifted(applied[levels:], "tm", -1)
            r_dual = -(dual_model - backward) - adjoint_field
            upward = r_dual + shifted(decay_field * r_dual, "tm", -1)

        obs_dual = obs_dual + (observed - obs_error * obs_dual - obs_image) / obs_error
        r_model = rhs_field - err_field * dual_model - (increment - forward)
        source = r_model - err_field * upward
        along = source
        along = source + decay_field * shifted(along, "tm", 1)
        dual_model = dual_model + upward
        increment = increment + along
    return (dual_model[None], obs_dual[None], increment[None])


def solution(mesh):
    in_specs = (
        P("tm", None, "space", None),
        P("tm", None, "space", None),
        P("tm", "space", None),
        P("tm", None, "space", None),
        P("tm", None, "space", None),
        P("tm", None, "space", None),
        P(None, "space", None),
        P(),
        P("tm", "space"),
        P("tm", "space", None),
        P("tm", "space", None, None),
        P("tm", "space", None),
        P("tm", "space", None),
    )
    out_specs = (P("tm", None, "space", None), P("tm", "space", None), P("tm", None, "space", None))
    return jax.shard_map(
        on_device, mesh=mesh, in_specs=in_specs, out_specs=out_specs, check_vma=False
    )
```

```python
import jax
import jax.numpy as jnp
from jax import lax
from jax.sharding import PartitionSpec as P

SUBSTEPS = 2
ITERS = 2
LANES = 128


def with_halo(cells, axis, dim, width):
    count = lax.axis_size(axis)
    ends = count - 1
    head = lax.slice_in_dim(cells, 0, width, axis=dim)
    tail = lax.slice_in_dim(cells, cells.shape[dim] - width, cells.shape[dim], axis=dim)
    flat = (-1, cells.shape[-1])
    from_prev = lax.ppermute(tail.reshape(flat), axis, [(i, i + 1) for i in range(ends)])
    from_next = lax.ppermute(head.reshape(flat), axis, [(i + 1, i) for i in range(ends)])
    return jnp.concatenate(
        [from_prev.reshape(tail.shape), cells, from_next.reshape(head.shape)], axis=dim
    )


def shifted(value, axis, by):
    length = lax.axis_size(axis)
    pairs = [(i, i + by) for i in range(length) if 0 <= i + by < length]
    return lax.ppermute(value, axis, pairs)


def model_apply(current, scaling_ext, diff_coef):
    for step in range(SUBSTEPS):
        gain = scaling_ext[:, step : scaling_ext.shape[1] - step]
        scaled = gain * current
        inner = scaled[:, 1:-1]
        laplace = (
            scaled[:, 2:]
            + scaled[:, :-2]
            + jnp.roll(inner, 1, 2)
            + jnp.roll(inner, -1, 2)
            - 4.0 * inner
        )
        current = gain[:, 1:-1] * (inner + diff_coef * laplace)
    return current


def gather_cols(fields, row_oh, col_oh, group_mask):
    levels, row_count, col_count = fields.shape
    slots, lanes, touched = col_oh.shape
    groups = col_count // lanes
    lines = jnp.einsum(
        "sr,lrc->slc", row_oh, fields.astype(jnp.bfloat16), preferred_element_type=jnp.float32
    ).astype(jnp.bfloat16)
    lines = lines.reshape(slots, levels, groups, lanes)
    picked = jnp.einsum("slab,sbj->slaj", lines, col_oh, preferred_element_type=jnp.float32)
    picked = jnp.sum(picked * group_mask[:, None, :, :], axis=2)
    return picked.astype(jnp.bfloat16)


def spread_cols(values, row_oh, col_oh, group_mask, levels, col_count):
    slots, lanes, touched = col_oh.shape
    groups = col_count // lanes
    row_count = row_oh.shape[1]
    grads = values.reshape(slots, levels, 1, touched)
    placed = grads * group_mask[:, None, :, :].astype(jnp.bfloat16)
    lines = jnp.einsum("slaj,sbj->slab", placed, col_oh, preferred_element_type=jnp.float32)
    total = jnp.einsum(
        "sr,slab->lrab", row_oh, lines.astype(jnp.bfloat16), preferred_element_type=jnp.float32
    )
    return total.reshape(levels, row_count, groups * lanes)


def on_device(
    increment_start,
    dual_model_start,
    dual_obs_start,
    model_rhs,
    err_var,
    decays,
    scaling,
    diffusion,
    owners,
    tile_cols,
    jacobian,
    innovation,
    obs_var,
):
    increment = increment_start[0]
    dual_model = dual_model_start[0]
    rhs_field = model_rhs[0]
    err_field = err_var[0]
    decay_field = decays[0]
    owner_list = owners[0]
    cell_index = tile_cols[0]
    observed = innovation[0].astype(jnp.float32)
    obs_error = obs_var[0].astype(jnp.float32)
    obs_dual = dual_obs_start[0].astype(jnp.float32)
    levels, row_count, col_count = increment.shape
    tiles_here, orows, touch_levels = jacobian.shape[1:]
    touched = touch_levels // levels
    owners_count = lax.axis_size("space")
    tm_count = lax.axis_size("tm")
    tm_here = lax.axis_index("tm")
    capacity = max(2, 2 * tiles_here // owners_count)
    slots_all = owners_count * capacity
    groups = col_count // LANES
    diff_coef = diffusion[:, None, None]

    jac_tiles = jacobian[0]

    one_hot = (owner_list[:, None] == jnp.arange(owners_count, dtype=jnp.int32)[None, :]).astype(
        jnp.int32
    )
    earlier_count = jnp.cumsum(one_hot, axis=0) - one_hot
    slot_rank = jnp.sum(earlier_count * one_hot, axis=1)
    position = owner_list * capacity + slot_rank
    slot_oh = (position[:, None] == jnp.arange(slots_all, dtype=jnp.int32)[None, :]).astype(
        jnp.bfloat16
    )
    packed_cells = jnp.zeros((slots_all, touched), jnp.int32).at[position].set(cell_index)
    requests = lax.all_to_all(
        packed_cells.reshape(owners_count, capacity, touched),
        "space",
        split_axis=0,
        concat_axis=0,
        tiled=True,
    ).reshape(slots_all, touched)
    req_rows = requests[:, 0] // col_count
    req_cols = requests % col_count
    row_oh = (req_rows[:, None] == jnp.arange(row_count, dtype=jnp.int32)[None, :])
    col_oh = (
        (req_cols % LANES)[:, None, :] == jnp.arange(LANES, dtype=jnp.int32)[None, :, None]
    ).astype(jnp.bfloat16)
    group_mask = (
        (req_cols // LANES)[:, None, :] == jnp.arange(groups, dtype=jnp.int32)[None, :, None]
    ).astype(jnp.float32)

    scaling_ext = None
    is_first = (tm_here == 0).astype(jnp.float32)
    is_last = (tm_here == tm_count - 1).astype(jnp.float32)

    for repeat in range(ITERS):
        wanted = gather_cols(increment, row_oh.astype(jnp.bfloat16), col_oh, group_mask)
        tile_grad = jnp.einsum(
            "toj,to->tj", jac_tiles, obs_dual.astype(jnp.bfloat16), preferred_element_type=jnp.float32
        ).astype(jnp.bfloat16)
        sent_grad = jnp.einsum(
            "ts,tjl->slj",
            slot_oh,
            tile_grad.reshape(tiles_here, touched, levels),
            preferred_element_type=jnp.float32,
        ).astype(jnp.bfloat16)
        both = jnp.stack(
            [
                wanted.reshape(owners_count, capacity * levels, touched),
                sent_grad.reshape(owners_count, capacity * levels, touched),
            ],
            axis=1,
        )
        got = lax.all_to_all(both, "space", split_axis=0, concat_axis=0, tiled=True)
        got_cols = got[:, 0].reshape(slots_all, touch_levels)
        got_grad = got[:, 1].reshape(slots_all, touch_levels)
        own_cols = jnp.einsum(
            "ts,slj->tjl",
            slot_oh,
            got_cols.reshape(slots_all, levels, touched),
            preferred_element_type=jnp.float32,
        ).astype(jnp.bfloat16).reshape(tiles_here, touch_levels)
        obs_image = jnp.einsum(
            "toj,tj->to", jac_tiles, own_cols, preferred_element_type=jnp.float32
        )
        adjoint_field = spread_cols(
            got_grad, row_oh.astype(jnp.bfloat16), col_oh, group_mask, levels, col_count
        )

        if tm_count == 2:
            chosen = jnp.where(tm_here == 0, increment, dual_model)
            if scaling_ext is None:
                both_ext = with_halo(jnp.stack([scaling, chosen]), "space", 2, SUBSTEPS)
                scaling_ext, chosen_ext = both_ext[0], both_ext[1]
            else:
                chosen_ext = with_halo(chosen, "space", 1, SUBSTEPS)
            applied = model_apply(chosen_ext, scaling_ext, diff_coef)
            other = lax.ppermute(applied, "tm", [(0, 1), (1, 0)])
            forward = other * (1.0 - is_first)
            backward = other * (1.0 - is_last)
            r_dual = -(dual_model - backward) - adjoint_field
            upward = r_dual + shifted(decay_field * r_dual, "tm", -1)
        else:
            if scaling_ext is None:
                scaling_ext = with_halo(scaling, "space", 1, SUBSTEPS)
            stacked = jnp.stack([increment, dual_model]).reshape(2 * levels, row_count, col_count)
            applied = model_apply(
                with_halo(stacked, "space", 1, SUBSTEPS),
                jnp.concatenate([scaling_ext, scaling_ext]),
                jnp.concatenate([diff_coef, diff_coef]),
            )
            forward = shifted(applied[:levels], "tm", 1)
            backward = shifted(applied[levels:], "tm", -1)
            r_dual = -(dual_model - backward) - adjoint_field
            upward = r_dual + shifted(decay_field * r_dual, "tm", -1)

        obs_dual = obs_dual + (observed - obs_error * obs_dual - obs_image) / obs_error
        r_model = rhs_field - err_field * dual_model - (increment - forward)
        source = r_model - err_field * upward
        along = source
        along = source + decay_field * shifted(along, "tm", 1)
        dual_model = dual_model + upward
        increment = increment + along
    return (dual_model[None], obs_dual[None], increment[None])


def solution(mesh):
    in_specs = (
        P("tm", None, "space", None),
        P("tm", None, "space", None),
        P("tm", "space", None),
        P("tm", None, "space", None),
        P("tm", None, "space", None),
        P("tm", None, "space", None),
        P(None, "space", None),
        P(),
        P("tm", "space"),
        P("tm", "space", None),
        P("tm", "space", None, None),
        P("tm", "space", None),
        P("tm", "space", None),
    )
    out_specs = (P("tm", None, "space", None), P("tm", "space", None), P("tm", None, "space", None))
    return jax.shard_map(
        on_device, mesh=mesh, in_specs=in_specs, out_specs=out_specs, check_vma=False
    )
```

```python
import jax
import jax.numpy as jnp
from jax import lax
from jax.sharding import PartitionSpec as P

SUBSTEPS = 2
ITERS = 2
LANES = 128


def with_halo(cells, axis, dim, width):
    count = lax.axis_size(axis)
    ends = count - 1
    head = lax.slice_in_dim(cells, 0, width, axis=dim)
    tail = lax.slice_in_dim(cells, cells.shape[dim] - width, cells.shape[dim], axis=dim)
    return jnp.concatenate(
        [
            lax.ppermute(tail, axis, [(i, i + 1) for i in range(ends)]),
            cells,
            lax.ppermute(head, axis, [(i + 1, i) for i in range(ends)]),
        ],
        axis=dim,
    )


def shifted(value, axis, by):
    length = lax.axis_size(axis)
    pairs = [(i, i + by) for i in range(length) if 0 <= i + by < length]
    return lax.ppermute(value, axis, pairs)


def model_apply(current, scaling_ext, diff_coef):
    for step in range(SUBSTEPS):
        gain = scaling_ext[:, step : scaling_ext.shape[1] - step]
        scaled = gain * current
        inner = scaled[:, 1:-1]
        laplace = (
            scaled[:, 2:]
            + scaled[:, :-2]
            + jnp.roll(inner, 1, 2)
            + jnp.roll(inner, -1, 2)
            - 4.0 * inner
        )
        current = gain[:, 1:-1] * (inner + diff_coef * laplace)
    return current


def gather_cols(fields, row_oh, col_oh, group_mask):
    levels, row_count, col_count = fields.shape
    slots, lanes, touched = col_oh.shape
    groups = col_count // lanes
    lines = jnp.einsum(
        "sr,lrc->slc", row_oh, fields.astype(jnp.bfloat16), preferred_element_type=jnp.float32
    ).astype(jnp.bfloat16)
    lines = lines.reshape(slots, levels, groups, lanes)
    picked = jnp.einsum("slab,sbj->slaj", lines, col_oh, preferred_element_type=jnp.float32)
    picked = jnp.sum(picked * group_mask[:, None, :, :], axis=2)
    return picked.astype(jnp.bfloat16)


def spread_cols(values, row_oh, col_oh, group_mask, levels, col_count):
    slots, lanes, touched = col_oh.shape
    groups = col_count // lanes
    row_count = row_oh.shape[1]
    grads = values.reshape(slots, levels, 1, touched)
    placed = grads * group_mask[:, None, :, :].astype(jnp.bfloat16)
    lines = jnp.einsum("slaj,sbj->slab", placed, col_oh, preferred_element_type=jnp.float32)
    total = jnp.einsum(
        "sr,slab->lrab", row_oh, lines.astype(jnp.bfloat16), preferred_element_type=jnp.float32
    )
    return total.reshape(levels, row_count, groups * lanes)


def on_device(
    increment_start,
    dual_model_start,
    dual_obs_start,
    model_rhs,
    err_var,
    decays,
    scaling,
    diffusion,
    owners,
    tile_cols,
    jacobian,
    innovation,
    obs_var,
):
    increment = increment_start[0]
    dual_model = dual_model_start[0]
    rhs_field = model_rhs[0]
    err_field = err_var[0]
    decay_field = decays[0]
    owner_list = owners[0]
    cell_index = tile_cols[0]
    observed = innovation[0].astype(jnp.float32)
    obs_error = obs_var[0].astype(jnp.float32)
    obs_dual = dual_obs_start[0].astype(jnp.float32)
    levels, row_count, col_count = increment.shape
    tiles_here, orows, touch_levels = jacobian.shape[1:]
    touched = touch_levels // levels
    owners_count = lax.axis_size("space")
    tm_count = lax.axis_size("tm")
    tm_here = lax.axis_index("tm")
    capacity = max(2, 2 * tiles_here // owners_count)
    slots_all = owners_count * capacity
    groups = col_count // LANES
    diff_coef = diffusion[:, None, None]

    jac_tiles = jacobian[0]

    one_hot = (owner_list[:, None] == jnp.arange(owners_count, dtype=jnp.int32)[None, :]).astype(
        jnp.int32
    )
    earlier_count = jnp.cumsum(one_hot, axis=0) - one_hot
    slot_rank = jnp.sum(earlier_count * one_hot, axis=1)
    position = owner_list * capacity + slot_rank
    slot_oh = (position[:, None] == jnp.arange(slots_all, dtype=jnp.int32)[None, :]).astype(
        jnp.bfloat16
    )
    packed_cells = jnp.zeros((slots_all, touched), jnp.int32).at[position].set(cell_index)
    requests = lax.all_to_all(
        packed_cells.reshape(owners_count, capacity, touched),
        "space",
        split_axis=0,
        concat_axis=0,
        tiled=True,
    ).reshape(slots_all, touched)
    req_rows = requests[:, 0] // col_count
    req_cols = requests % col_count
    row_oh = (req_rows[:, None] == jnp.arange(row_count, dtype=jnp.int32)[None, :])
    col_oh = (
        (req_cols % LANES)[:, None, :] == jnp.arange(LANES, dtype=jnp.int32)[None, :, None]
    ).astype(jnp.bfloat16)
    group_mask = (
        (req_cols // LANES)[:, None, :] == jnp.arange(groups, dtype=jnp.int32)[None, :, None]
    ).astype(jnp.float32)

    scaling_ext = None
    is_first = (tm_here == 0).astype(jnp.float32)
    is_last = (tm_here == tm_count - 1).astype(jnp.float32)

    for repeat in range(ITERS):
        wanted = gather_cols(increment, row_oh.astype(jnp.bfloat16), col_oh, group_mask)
        tile_grad = jnp.einsum(
            "toj,to->tj", jac_tiles, obs_dual.astype(jnp.bfloat16), preferred_element_type=jnp.float32
        ).astype(jnp.bfloat16)
        sent_grad = jnp.einsum(
            "ts,tjl->slj",
            slot_oh,
            tile_grad.reshape(tiles_here, touched, levels),
            preferred_element_type=jnp.float32,
        ).astype(jnp.bfloat16)
        both = jnp.concatenate(
            [
                wanted.reshape(owners_count, capacity * levels, touched),
                sent_grad.reshape(owners_count, capacity * levels, touched),
            ],
            axis=2,
        )
        got = lax.all_to_all(both, "space", split_axis=0, concat_axis=0, tiled=True)
        got_cols = got[:, :, :touched].reshape(slots_all, touch_levels)
        got_grad = got[:, :, touched:].reshape(slots_all, touch_levels)
        own_cols = jnp.einsum(
            "ts,slj->tjl",
            slot_oh,
            got_cols.reshape(slots_all, levels, touched),
            preferred_element_type=jnp.float32,
        ).astype(jnp.bfloat16).reshape(tiles_here, touch_levels)
        obs_image = jnp.einsum(
            "toj,tj->to", jac_tiles, own_cols, preferred_element_type=jnp.float32
        )
        adjoint_field = spread_cols(
            got_grad, row_oh.astype(jnp.bfloat16), col_oh, group_mask, levels, col_count
        )

        if tm_count == 2:
            chosen = jnp.where(tm_here == 0, increment, dual_model)
            if scaling_ext is None:
                both_ext = with_halo(jnp.stack([scaling, chosen]), "space", 2, SUBSTEPS)
                scaling_ext, chosen_ext = both_ext[0], both_ext[1]
            else:
                chosen_ext = with_halo(chosen, "space", 1, SUBSTEPS)
            applied = model_apply(chosen_ext, scaling_ext, diff_coef)
            other = lax.ppermute(applied, "tm", [(0, 1), (1, 0)])
            forward = other * (1.0 - is_first)
            backward = other * (1.0 - is_last)
            r_dual = -(dual_model - backward) - adjoint_field
            upward = r_dual + shifted(decay_field * r_dual, "tm", -1)
        else:
            if scaling_ext is None:
                scaling_ext = with_halo(scaling, "space", 1, SUBSTEPS)
            stacked = jnp.stack([increment, dual_model]).reshape(2 * levels, row_count, col_count)
            applied = model_apply(
                with_halo(stacked, "space", 1, SUBSTEPS),
                jnp.concatenate([scaling_ext, scaling_ext]),
                jnp.concatenate([diff_coef, diff_coef]),
            )
            forward = shifted(applied[:levels], "tm", 1)
            backward = shifted(applied[levels:], "tm", -1)
            r_dual = -(dual_model - backward) - adjoint_field
            upward = r_dual + shifted(decay_field * r_dual, "tm", -1)

        obs_dual = obs_dual + (observed - obs_error * obs_dual - obs_image) / obs_error
        r_model = rhs_field - err_field * dual_model - (increment - forward)
        source = r_model - err_field * upward
        along = source
        along = source + decay_field * shifted(along, "tm", 1)
        dual_model = dual_model + upward
        increment = increment + along
    return (dual_model[None], obs_dual[None], increment[None])


def solution(mesh):
    in_specs = (
        P("tm", None, "space", None),
        P("tm", None, "space", None),
        P("tm", "space", None),
        P("tm", None, "space", None),
        P("tm", None, "space", None),
        P("tm", None, "space", None),
        P(None, "space", None),
        P(),
        P("tm", "space"),
        P("tm", "space", None),
        P("tm", "space", None, None),
        P("tm", "space", None),
        P("tm", "space", None),
    )
    out_specs = (P("tm", None, "space", None), P("tm", "space", None), P("tm", None, "space", None))
    return jax.shard_map(
        on_device, mesh=mesh, in_specs=in_specs, out_specs=out_specs, check_vma=False
    )
```

```python
import jax
import jax.numpy as jnp
from jax import lax
from jax.sharding import PartitionSpec as P

SUBSTEPS = 2
ITERS = 2
LANES = 128


def with_halo(cells, axis, dim, width):
    count = lax.axis_size(axis)
    ends = count - 1
    head = lax.slice_in_dim(cells, 0, width, axis=dim)
    tail = lax.slice_in_dim(cells, cells.shape[dim] - width, cells.shape[dim], axis=dim)
    return jnp.concatenate(
        [
            lax.ppermute(tail, axis, [(i, i + 1) for i in range(ends)]),
            cells,
            lax.ppermute(head, axis, [(i + 1, i) for i in range(ends)]),
        ],
        axis=dim,
    )


def shifted(value, axis, by):
    length = lax.axis_size(axis)
    pairs = [(i, i + by) for i in range(length) if 0 <= i + by < length]
    return lax.ppermute(value, axis, pairs)


def model_apply(current, scaling_ext, diff_coef):
    for step in range(SUBSTEPS):
        gain = scaling_ext[:, step : scaling_ext.shape[1] - step]
        scaled = gain * current
        inner = scaled[:, 1:-1]
        laplace = (
            scaled[:, 2:]
            + scaled[:, :-2]
            + jnp.roll(inner, 1, 2)
            + jnp.roll(inner, -1, 2)
            - 4.0 * inner
        )
        current = gain[:, 1:-1] * (inner + diff_coef * laplace)
    return current


def gather_cols(fields, row_oh, col_oh, group_mask):
    levels, row_count, col_count = fields.shape
    slots, lanes, touched = col_oh.shape
    groups = col_count // lanes
    lines = jnp.einsum(
        "sr,lrc->slc", row_oh, fields.astype(jnp.bfloat16), preferred_element_type=jnp.float32
    ).astype(jnp.bfloat16)
    lines = lines.reshape(slots, levels, groups, lanes)
    picked = jnp.einsum("slab,sbj->slaj", lines, col_oh, preferred_element_type=jnp.float32)
    picked = jnp.sum(picked * group_mask[:, None, :, :], axis=2)
    return picked.astype(jnp.bfloat16)


def spread_cols(values, row_oh, col_oh, group_mask, levels, col_count):
    slots, lanes, touched = col_oh.shape
    groups = col_count // lanes
    row_count = row_oh.shape[1]
    grads = values.reshape(slots, levels, 1, touched)
    placed = grads * group_mask[:, None, :, :].astype(jnp.bfloat16)
    lines = jnp.einsum("slaj,sbj->slab", placed, col_oh, preferred_element_type=jnp.float32)
    total = jnp.einsum(
        "sr,slab->lrab", row_oh, lines.astype(jnp.bfloat16), preferred_element_type=jnp.float32
    )
    return total.reshape(levels, row_count, groups * lanes)


def on_device(
    increment_start,
    dual_model_start,
    dual_obs_start,
    model_rhs,
    err_var,
    decays,
    scaling,
    diffusion,
    owners,
    tile_cols,
    jacobian,
    innovation,
    obs_var,
):
    increment = increment_start[0]
    dual_model = dual_model_start[0]
    rhs_field = model_rhs[0]
    err_field = err_var[0]
    decay_field = decays[0]
    owner_list = owners[0]
    cell_index = tile_cols[0]
    observed = innovation[0].astype(jnp.float32)
    obs_error = obs_var[0].astype(jnp.float32)
    obs_dual = dual_obs_start[0].astype(jnp.float32)
    levels, row_count, col_count = increment.shape
    tiles_here, orows, touch_levels = jacobian.shape[1:]
    touched = touch_levels // levels
    owners_count = lax.axis_size("space")
    tm_count = lax.axis_size("tm")
    tm_here = lax.axis_index("tm")
    capacity = max(2, 2 * tiles_here // owners_count)
    slots_all = owners_count * capacity
    groups = col_count // LANES
    diff_coef = diffusion[:, None, None]

    jac_tiles = jacobian[0]

    one_hot = (owner_list[:, None] == jnp.arange(owners_count, dtype=jnp.int32)[None, :]).astype(
        jnp.int32
    )
    earlier_count = jnp.cumsum(one_hot, axis=0) - one_hot
    slot_rank = jnp.sum(earlier_count * one_hot, axis=1)
    position = owner_list * capacity + slot_rank
    slot_oh = (position[:, None] == jnp.arange(slots_all, dtype=jnp.int32)[None, :]).astype(
        jnp.bfloat16
    )
    packed_cells = jnp.zeros((slots_all, touched), jnp.int32).at[position].set(cell_index)
    requests = lax.all_to_all(
        packed_cells.reshape(owners_count, capacity, touched),
        "space",
        split_axis=0,
        concat_axis=0,
        tiled=True,
    ).reshape(slots_all, touched)
    req_rows = requests[:, 0] // col_count
    req_cols = requests % col_count
    row_oh = (req_rows[:, None] == jnp.arange(row_count, dtype=jnp.int32)[None, :])
    col_oh = (
        (req_cols % LANES)[:, None, :] == jnp.arange(LANES, dtype=jnp.int32)[None, :, None]
    ).astype(jnp.bfloat16)
    group_mask = (
        (req_cols // LANES)[:, None, :] == jnp.arange(groups, dtype=jnp.int32)[None, :, None]
    ).astype(jnp.float32)

    scaling_ext = None
    is_first = (tm_here == 0).astype(jnp.float32)
    is_last = (tm_here == tm_count - 1).astype(jnp.float32)

    for repeat in range(ITERS):
        wanted = gather_cols(increment, row_oh.astype(jnp.bfloat16), col_oh, group_mask)
        tile_grad = jnp.einsum(
            "toj,to->tj", jac_tiles, obs_dual.astype(jnp.bfloat16), preferred_element_type=jnp.float32
        ).astype(jnp.bfloat16)
        sent_grad = jnp.einsum(
            "ts,tjl->slj",
            slot_oh,
            tile_grad.reshape(tiles_here, touched, levels),
            preferred_element_type=jnp.float32,
        ).astype(jnp.bfloat16)
        both = jnp.concatenate(
            [
                wanted.reshape(owners_count, capacity * levels, touched),
                sent_grad.reshape(owners_count, capacity * levels, touched),
            ],
            axis=2,
        )
        got = lax.all_to_all(both, "space", split_axis=0, concat_axis=0, tiled=True)
        got_cols = got[:, :, :touched].reshape(slots_all, touch_levels)
        got_grad = got[:, :, touched:].reshape(slots_all, touch_levels)
        own_cols = jnp.einsum(
            "ts,slj->tjl",
            slot_oh,
            got_cols.reshape(slots_all, levels, touched),
            preferred_element_type=jnp.float32,
        ).astype(jnp.bfloat16).reshape(tiles_here, touch_levels)
        obs_image = jnp.einsum(
            "toj,tj->to", jac_tiles, own_cols, preferred_element_type=jnp.float32
        )
        adjoint_field = spread_cols(
            got_grad, row_oh.astype(jnp.bfloat16), col_oh, group_mask, levels, col_count
        )

        if tm_count == 2:
            chosen = jnp.where(tm_here == 0, increment, dual_model)
            if scaling_ext is None:
                both_ext = with_halo(jnp.stack([scaling, chosen]), "space", 2, SUBSTEPS)
                scaling_ext, chosen_ext = both_ext[0], both_ext[1]
            else:
                chosen_ext = with_halo(chosen, "space", 1, SUBSTEPS)
            applied = model_apply(chosen_ext, scaling_ext, diff_coef)
            other = lax.ppermute(applied, "tm", [(0, 1), (1, 0)])
            forward = other * (1.0 - is_first)
            backward = other * (1.0 - is_last)
            r_dual = -(dual_model - backward) - adjoint_field
            decayed = decay_field * r_dual
            if repeat == ITERS - 1:
                own_cols, decayed = lax.optimization_barrier((own_cols, decayed))
                obs_image = jnp.einsum(
                    "toj,tj->to", jac_tiles, own_cols, preferred_element_type=jnp.float32
                )
            upward = r_dual + shifted(decayed, "tm", -1)
        else:
            if scaling_ext is None:
                scaling_ext = with_halo(scaling, "space", 1, SUBSTEPS)
            stacked = jnp.stack([increment, dual_model]).reshape(2 * levels, row_count, col_count)
            applied = model_apply(
                with_halo(stacked, "space", 1, SUBSTEPS),
                jnp.concatenate([scaling_ext, scaling_ext]),
                jnp.concatenate([diff_coef, diff_coef]),
            )
            forward = shifted(applied[:levels], "tm", 1)
            backward = shifted(applied[levels:], "tm", -1)
            r_dual = -(dual_model - backward) - adjoint_field
            upward = r_dual + shifted(decay_field * r_dual, "tm", -1)

        obs_dual = obs_dual + (observed - obs_error * obs_dual - obs_image) / obs_error
        r_model = rhs_field - err_field * dual_model - (increment - forward)
        source = r_model - err_field * upward
        along = source
        along = source + decay_field * shifted(along, "tm", 1)
        dual_model = dual_model + upward
        increment = increment + along
    return (dual_model[None], obs_dual[None], increment[None])


def solution(mesh):
    in_specs = (
        P("tm", None, "space", None),
        P("tm", None, "space", None),
        P("tm", "space", None),
        P("tm", None, "space", None),
        P("tm", None, "space", None),
        P("tm", None, "space", None),
        P(None, "space", None),
        P(),
        P("tm", "space"),
        P("tm", "space", None),
        P("tm", "space", None, None),
        P("tm", "space", None),
        P("tm", "space", None),
    )
    out_specs = (P("tm", None, "space", None), P("tm", "space", None), P("tm", None, "space", None))
    return jax.shard_map(
        on_device, mesh=mesh, in_specs=in_specs, out_specs=out_specs, check_vma=False
    )
```

```python
import jax
import jax.numpy as jnp
from jax import lax
from jax.sharding import PartitionSpec as P

SUBSTEPS = 2
ITERS = 2
LANES = 128


def with_halo(cells, axis, dim, width):
    count = lax.axis_size(axis)
    ends = count - 1
    head = lax.slice_in_dim(cells, 0, width, axis=dim)
    tail = lax.slice_in_dim(cells, cells.shape[dim] - width, cells.shape[dim], axis=dim)
    return jnp.concatenate(
        [
            lax.ppermute(tail, axis, [(i, i + 1) for i in range(ends)]),
            cells,
            lax.ppermute(head, axis, [(i + 1, i) for i in range(ends)]),
        ],
        axis=dim,
    )


def shifted(value, axis, by):
    length = lax.axis_size(axis)
    pairs = [(i, i + by) for i in range(length) if 0 <= i + by < length]
    return lax.ppermute(value, axis, pairs)


def model_apply(current, scaling_ext, diff_coef):
    for step in range(SUBSTEPS):
        gain = scaling_ext[:, step : scaling_ext.shape[1] - step]
        scaled = gain * current
        inner = scaled[:, 1:-1]
        laplace = (
            scaled[:, 2:]
            + scaled[:, :-2]
            + jnp.roll(inner, 1, 2)
            + jnp.roll(inner, -1, 2)
            - 4.0 * inner
        )
        current = gain[:, 1:-1] * (inner + diff_coef * laplace)
    return current


def gather_cols(fields, row_oh, col_oh, group_mask):
    levels, row_count, col_count = fields.shape
    slots, lanes, touched = col_oh.shape
    groups = col_count // lanes
    lines = jnp.einsum(
        "sr,lrc->slc", row_oh, fields.astype(jnp.bfloat16), preferred_element_type=jnp.float32
    ).astype(jnp.bfloat16)
    lines = lines.reshape(slots, levels, groups, lanes)
    picked = jnp.einsum("slab,sbj->slaj", lines, col_oh, preferred_element_type=jnp.bfloat16)
    return jnp.sum(picked * group_mask[:, None, :, :].astype(jnp.bfloat16), axis=2)


def spread_cols(values, row_oh, col_oh, group_mask, levels, col_count):
    slots, lanes, touched = col_oh.shape
    groups = col_count // lanes
    row_count = row_oh.shape[1]
    grads = values.reshape(slots, levels, 1, touched)
    placed = grads * group_mask[:, None, :, :].astype(jnp.bfloat16)
    lines = jnp.einsum("slaj,sbj->slab", placed, col_oh, preferred_element_type=jnp.float32)
    total = jnp.einsum(
        "sr,slab->lrab", row_oh, lines.astype(jnp.bfloat16), preferred_element_type=jnp.float32
    )
    return total.reshape(levels, row_count, groups * lanes)


def on_device(
    increment_start,
    dual_model_start,
    dual_obs_start,
    model_rhs,
    err_var,
    decays,
    scaling,
    diffusion,
    owners,
    tile_cols,
    jacobian,
    innovation,
    obs_var,
):
    increment = increment_start[0]
    dual_model = dual_model_start[0]
    rhs_field = model_rhs[0]
    err_field = err_var[0]
    decay_field = decays[0]
    owner_list = owners[0]
    cell_index = tile_cols[0]
    observed = innovation[0].astype(jnp.float32)
    obs_error = obs_var[0].astype(jnp.float32)
    obs_dual = dual_obs_start[0].astype(jnp.float32)
    levels, row_count, col_count = increment.shape
    tiles_here, orows, touch_levels = jacobian.shape[1:]
    touched = touch_levels // levels
    owners_count = lax.axis_size("space")
    tm_count = lax.axis_size("tm")
    tm_here = lax.axis_index("tm")
    capacity = max(2, 2 * tiles_here // owners_count)
    slots_all = owners_count * capacity
    groups = col_count // LANES
    diff_coef = diffusion[:, None, None]

    jac_tiles = jacobian[0]

    one_hot = (owner_list[:, None] == jnp.arange(owners_count, dtype=jnp.int32)[None, :]).astype(
        jnp.int32
    )
    earlier_count = jnp.cumsum(one_hot, axis=0) - one_hot
    slot_rank = jnp.sum(earlier_count * one_hot, axis=1)
    position = owner_list * capacity + slot_rank
    slot_oh = (position[:, None] == jnp.arange(slots_all, dtype=jnp.int32)[None, :]).astype(
        jnp.bfloat16
    )
    packed_cells = jnp.zeros((slots_all, touched), jnp.int32).at[position].set(cell_index)
    requests = lax.all_to_all(
        packed_cells.reshape(owners_count, capacity, touched),
        "space",
        split_axis=0,
        concat_axis=0,
        tiled=True,
    ).reshape(slots_all, touched)
    req_rows = requests[:, 0] // col_count
    req_cols = requests % col_count
    row_oh = (req_rows[:, None] == jnp.arange(row_count, dtype=jnp.int32)[None, :])
    col_oh = (
        (req_cols % LANES)[:, None, :] == jnp.arange(LANES, dtype=jnp.int32)[None, :, None]
    ).astype(jnp.bfloat16)
    group_mask = (
        (req_cols // LANES)[:, None, :] == jnp.arange(groups, dtype=jnp.int32)[None, :, None]
    ).astype(jnp.float32)

    scaling_ext = None
    is_first = (tm_here == 0).astype(jnp.float32)
    is_last = (tm_here == tm_count - 1).astype(jnp.float32)

    for repeat in range(ITERS):
        wanted = gather_cols(increment, row_oh.astype(jnp.bfloat16), col_oh, group_mask)
        tile_grad = jnp.einsum(
            "toj,to->tj", jac_tiles, obs_dual.astype(jnp.bfloat16), preferred_element_type=jnp.float32
        ).astype(jnp.bfloat16)
        sent_grad = jnp.einsum(
            "ts,tjl->slj",
            slot_oh,
            tile_grad.reshape(tiles_here, touched, levels),
            preferred_element_type=jnp.float32,
        ).astype(jnp.bfloat16)
        both = jnp.concatenate(
            [
                wanted.reshape(owners_count, capacity * levels, touched),
                sent_grad.reshape(owners_count, capacity * levels, touched),
            ],
            axis=2,
        )
        got = lax.all_to_all(both, "space", split_axis=0, concat_axis=0, tiled=True)
        got_cols = got[:, :, :touched].reshape(slots_all, touch_levels)
        got_grad = got[:, :, touched:].reshape(slots_all, touch_levels)
        own_cols = jnp.einsum(
            "ts,slj->tjl",
            slot_oh,
            got_cols.reshape(slots_all, levels, touched),
            preferred_element_type=jnp.float32,
        ).astype(jnp.bfloat16).reshape(tiles_here, touch_levels)
        obs_image = jnp.einsum(
            "toj,tj->to", jac_tiles, own_cols, preferred_element_type=jnp.float32
        )
        adjoint_field = spread_cols(
            got_grad, row_oh.astype(jnp.bfloat16), col_oh, group_mask, levels, col_count
        )

        if tm_count == 2:
            chosen = jnp.where(tm_here == 0, increment, dual_model)
            if scaling_ext is None:
                both_ext = with_halo(jnp.stack([scaling, chosen]), "space", 2, SUBSTEPS)
                scaling_ext, chosen_ext = both_ext[0], both_ext[1]
            else:
                chosen_ext = with_halo(chosen, "space", 1, SUBSTEPS)
            applied = model_apply(chosen_ext, scaling_ext, diff_coef)
            other = lax.ppermute(applied, "tm", [(0, 1), (1, 0)])
            forward = other * (1.0 - is_first)
            backward = other * (1.0 - is_last)
            r_dual = -(dual_model - backward) - adjoint_field
            decayed = decay_field * r_dual
            if repeat == ITERS - 1:
                own_cols, decayed = lax.optimization_barrier((own_cols, decayed))
                obs_image = jnp.einsum(
                    "toj,tj->to", jac_tiles, own_cols, preferred_element_type=jnp.float32
                )
            upward = r_dual + shifted(decayed, "tm", -1)
        else:
            if scaling_ext is None:
                scaling_ext = with_halo(scaling, "space", 1, SUBSTEPS)
            stacked = jnp.stack([increment, dual_model]).reshape(2 * levels, row_count, col_count)
            applied = model_apply(
                with_halo(stacked, "space", 1, SUBSTEPS),
                jnp.concatenate([scaling_ext, scaling_ext]),
                jnp.concatenate([diff_coef, diff_coef]),
            )
            forward = shifted(applied[:levels], "tm", 1)
            backward = shifted(applied[levels:], "tm", -1)
            r_dual = -(dual_model - backward) - adjoint_field
            upward = r_dual + shifted(decay_field * r_dual, "tm", -1)

        obs_dual = obs_dual + (observed - obs_error * obs_dual - obs_image) / obs_error
        r_model = rhs_field - err_field * dual_model - (increment - forward)
        source = r_model - err_field * upward
        along = source
        along = source + decay_field * shifted(along, "tm", 1)
        dual_model = dual_model + upward
        increment = increment + along
    return (dual_model[None], obs_dual[None], increment[None])


def solution(mesh):
    in_specs = (
        P("tm", None, "space", None),
        P("tm", None, "space", None),
        P("tm", "space", None),
        P("tm", None, "space", None),
        P("tm", None, "space", None),
        P("tm", None, "space", None),
        P(None, "space", None),
        P(),
        P("tm", "space"),
        P("tm", "space", None),
        P("tm", "space", None, None),
        P("tm", "space", None),
        P("tm", "space", None),
    )
    out_specs = (P("tm", None, "space", None), P("tm", "space", None), P("tm", None, "space", None))
    return jax.shard_map(
        on_device, mesh=mesh, in_specs=in_specs, out_specs=out_specs, check_vma=False
    )
```

```python
import jax
import jax.numpy as jnp
from jax import lax
from jax.sharding import PartitionSpec as P

SUBSTEPS = 2
ITERS = 2
LANES = 128


def with_halo(cells, axis, dim, width):
    count = lax.axis_size(axis)
    ends = count - 1
    head = lax.slice_in_dim(cells, 0, width, axis=dim)
    tail = lax.slice_in_dim(cells, cells.shape[dim] - width, cells.shape[dim], axis=dim)
    return jnp.concatenate(
        [
            lax.ppermute(tail, axis, [(i, i + 1) for i in range(ends)]),
            cells,
            lax.ppermute(head, axis, [(i + 1, i) for i in range(ends)]),
        ],
        axis=dim,
    )


def shifted(value, axis, by):
    length = lax.axis_size(axis)
    pairs = [(i, i + by) for i in range(length) if 0 <= i + by < length]
    return lax.ppermute(value, axis, pairs)


def model_apply(current, scaling_ext, diff_coef):
    for step in range(SUBSTEPS):
        gain = scaling_ext[:, step : scaling_ext.shape[1] - step]
        scaled = gain * current
        inner = scaled[:, 1:-1]
        laplace = (
            scaled[:, 2:]
            + scaled[:, :-2]
            + jnp.roll(inner, 1, 2)
            + jnp.roll(inner, -1, 2)
            - 4.0 * inner
        )
        current = gain[:, 1:-1] * (inner + diff_coef * laplace)
    return current


def gather_cols(fields, row_oh, col_oh, group_mask):
    levels, row_count, col_count = fields.shape
    slots, lanes, touched = col_oh.shape
    groups = col_count // lanes
    lines = jnp.einsum(
        "sr,lrc->slc", row_oh, fields.astype(jnp.bfloat16), preferred_element_type=jnp.float32
    ).astype(jnp.bfloat16)
    lines = lines.reshape(slots, levels, groups, lanes)
    picked = jnp.einsum("slab,sbj->slaj", lines, col_oh, preferred_element_type=jnp.bfloat16)
    return jnp.sum(picked * group_mask[:, None, :, :].astype(jnp.bfloat16), axis=2)


def spread_cols(values, row_oh, col_oh, group_mask, levels, col_count):
    slots, lanes, touched = col_oh.shape
    groups = col_count // lanes
    row_count = row_oh.shape[1]
    grads = values.reshape(slots, levels, 1, touched)
    placed = grads * group_mask[:, None, :, :].astype(jnp.bfloat16)
    lines = jnp.einsum("slaj,sbj->slab", placed, col_oh, preferred_element_type=jnp.bfloat16)
    total = jnp.einsum("sr,slab->lrab", row_oh, lines, preferred_element_type=jnp.float32)
    return total.reshape(levels, row_count, groups * lanes)


def on_device(
    increment_start,
    dual_model_start,
    dual_obs_start,
    model_rhs,
    err_var,
    decays,
    scaling,
    diffusion,
    owners,
    tile_cols,
    jacobian,
    innovation,
    obs_var,
):
    increment = increment_start[0]
    dual_model = dual_model_start[0]
    rhs_field = model_rhs[0]
    err_field = err_var[0]
    decay_field = decays[0]
    owner_list = owners[0]
    cell_index = tile_cols[0]
    observed = innovation[0].astype(jnp.float32)
    obs_error = obs_var[0].astype(jnp.float32)
    obs_dual = dual_obs_start[0].astype(jnp.float32)
    levels, row_count, col_count = increment.shape
    tiles_here, orows, touch_levels = jacobian.shape[1:]
    touched = touch_levels // levels
    owners_count = lax.axis_size("space")
    tm_count = lax.axis_size("tm")
    tm_here = lax.axis_index("tm")
    capacity = max(2, 2 * tiles_here // owners_count)
    slots_all = owners_count * capacity
    groups = col_count // LANES
    diff_coef = diffusion[:, None, None]

    jac_tiles = jacobian[0]

    one_hot = (owner_list[:, None] == jnp.arange(owners_count, dtype=jnp.int32)[None, :]).astype(
        jnp.int32
    )
    earlier_count = jnp.cumsum(one_hot, axis=0) - one_hot
    slot_rank = jnp.sum(earlier_count * one_hot, axis=1)
    position = owner_list * capacity + slot_rank
    slot_oh = (position[:, None] == jnp.arange(slots_all, dtype=jnp.int32)[None, :]).astype(
        jnp.bfloat16
    )
    packed_cells = jnp.zeros((slots_all, touched), jnp.int32).at[position].set(cell_index)
    requests = lax.all_to_all(
        packed_cells.reshape(owners_count, capacity, touched),
        "space",
        split_axis=0,
        concat_axis=0,
        tiled=True,
    ).reshape(slots_all, touched)
    req_rows = requests[:, 0] // col_count
    req_cols = requests % col_count
    row_oh = (req_rows[:, None] == jnp.arange(row_count, dtype=jnp.int32)[None, :])
    col_oh = (
        (req_cols % LANES)[:, None, :] == jnp.arange(LANES, dtype=jnp.int32)[None, :, None]
    ).astype(jnp.bfloat16)
    group_mask = (
        (req_cols // LANES)[:, None, :] == jnp.arange(groups, dtype=jnp.int32)[None, :, None]
    ).astype(jnp.float32)

    scaling_ext = None
    is_first = (tm_here == 0).astype(jnp.float32)
    is_last = (tm_here == tm_count - 1).astype(jnp.float32)

    for repeat in range(ITERS):
        wanted = gather_cols(increment, row_oh.astype(jnp.bfloat16), col_oh, group_mask)
        tile_grad = jnp.einsum(
            "toj,to->tj", jac_tiles, obs_dual.astype(jnp.bfloat16), preferred_element_type=jnp.float32
        ).astype(jnp.bfloat16)
        sent_grad = jnp.einsum(
            "ts,tjl->slj",
            slot_oh,
            tile_grad.reshape(tiles_here, touched, levels),
            preferred_element_type=jnp.float32,
        ).astype(jnp.bfloat16)
        both = jnp.concatenate(
            [
                wanted.reshape(owners_count, capacity * levels, touched),
                sent_grad.reshape(owners_count, capacity * levels, touched),
            ],
            axis=2,
        )
        got = lax.all_to_all(both, "space", split_axis=0, concat_axis=0, tiled=True)
        got_cols = got[:, :, :touched].reshape(slots_all, touch_levels)
        got_grad = got[:, :, touched:].reshape(slots_all, touch_levels)
        own_cols = jnp.einsum(
            "ts,slj->tjl",
            slot_oh,
            got_cols.reshape(slots_all, levels, touched),
            preferred_element_type=jnp.float32,
        ).astype(jnp.bfloat16).reshape(tiles_here, touch_levels)
        obs_image = jnp.einsum(
            "toj,tj->to", jac_tiles, own_cols, preferred_element_type=jnp.float32
        )
        adjoint_field = spread_cols(
            got_grad, row_oh.astype(jnp.bfloat16), col_oh, group_mask, levels, col_count
        )

        if tm_count == 2:
            chosen = jnp.where(tm_here == 0, increment, dual_model)
            if scaling_ext is None:
                both_ext = with_halo(jnp.stack([scaling, chosen]), "space", 2, SUBSTEPS)
                scaling_ext, chosen_ext = both_ext[0], both_ext[1]
            else:
                chosen_ext = with_halo(chosen, "space", 1, SUBSTEPS)
            applied = model_apply(chosen_ext, scaling_ext, diff_coef)
            other = lax.ppermute(applied, "tm", [(0, 1), (1, 0)])
            forward = other * (1.0 - is_first)
            backward = other * (1.0 - is_last)
            r_dual = -(dual_model - backward) - adjoint_field
            decayed = decay_field * r_dual
            if repeat == ITERS - 1:
                own_cols, decayed = lax.optimization_barrier((own_cols, decayed))
                obs_image = jnp.einsum(
                    "toj,tj->to", jac_tiles, own_cols, preferred_element_type=jnp.float32
                )
            upward = r_dual + shifted(decayed, "tm", -1)
        else:
            if scaling_ext is None:
                scaling_ext = with_halo(scaling, "space", 1, SUBSTEPS)
            stacked = jnp.stack([increment, dual_model]).reshape(2 * levels, row_count, col_count)
            applied = model_apply(
                with_halo(stacked, "space", 1, SUBSTEPS),
                jnp.concatenate([scaling_ext, scaling_ext]),
                jnp.concatenate([diff_coef, diff_coef]),
            )
            forward = shifted(applied[:levels], "tm", 1)
            backward = shifted(applied[levels:], "tm", -1)
            r_dual = -(dual_model - backward) - adjoint_field
            upward = r_dual + shifted(decay_field * r_dual, "tm", -1)

        obs_dual = obs_dual + (observed - obs_error * obs_dual - obs_image) / obs_error
        r_model = rhs_field - err_field * dual_model - (increment - forward)
        source = r_model - err_field * upward
        along = source
        along = source + decay_field * shifted(along, "tm", 1)
        dual_model = dual_model + upward
        increment = increment + along
    return (dual_model[None], obs_dual[None], increment[None])


def solution(mesh):
    in_specs = (
        P("tm", None, "space", None),
        P("tm", None, "space", None),
        P("tm", "space", None),
        P("tm", None, "space", None),
        P("tm", None, "space", None),
        P("tm", None, "space", None),
        P(None, "space", None),
        P(),
        P("tm", "space"),
        P("tm", "space", None),
        P("tm", "space", None, None),
        P("tm", "space", None),
        P("tm", "space", None),
    )
    out_specs = (P("tm", None, "space", None), P("tm", "space", None), P("tm", None, "space", None))
    return jax.shard_map(
        on_device, mesh=mesh, in_specs=in_specs, out_specs=out_specs, check_vma=False
    )
```

```python
import jax
import jax.numpy as jnp
from jax import lax
from jax.sharding import PartitionSpec as P

SUBSTEPS = 2
ITERS = 2
LANES = 128


def with_halo(cells, axis, dim, width):
    count = lax.axis_size(axis)
    ends = count - 1
    head = lax.slice_in_dim(cells, 0, width, axis=dim)
    tail = lax.slice_in_dim(cells, cells.shape[dim] - width, cells.shape[dim], axis=dim)
    return jnp.concatenate(
        [
            lax.ppermute(tail, axis, [(i, i + 1) for i in range(ends)]),
            cells,
            lax.ppermute(head, axis, [(i + 1, i) for i in range(ends)]),
        ],
        axis=dim,
    )


def shifted(value, axis, by):
    length = lax.axis_size(axis)
    pairs = [(i, i + by) for i in range(length) if 0 <= i + by < length]
    return lax.ppermute(value, axis, pairs)


def model_apply(current, scaling_ext, diff_coef):
    for step in range(SUBSTEPS):
        gain = scaling_ext[:, step : scaling_ext.shape[1] - step]
        scaled = gain * current
        inner = scaled[:, 1:-1]
        laplace = (
            scaled[:, 2:]
            + scaled[:, :-2]
            + jnp.roll(inner, 1, 2)
            + jnp.roll(inner, -1, 2)
            - 4.0 * inner
        )
        current = gain[:, 1:-1] * (inner + diff_coef * laplace)
    return current


def gather_cols(fields, row_oh, col_oh, group_mask):
    levels, row_count, col_count = fields.shape
    slots, lanes, touched = col_oh.shape
    groups = col_count // lanes
    lines = jnp.einsum(
        "sr,lrc->slc", row_oh, fields.astype(jnp.bfloat16), preferred_element_type=jnp.bfloat16
    )
    lines = lines.reshape(slots, levels, groups, lanes)
    picked = jnp.einsum("slab,sbj->slaj", lines, col_oh, preferred_element_type=jnp.bfloat16)
    return jnp.sum(picked * group_mask[:, None, :, :].astype(jnp.bfloat16), axis=2)


def spread_cols(values, row_oh, col_oh, group_mask, levels, col_count):
    slots, lanes, touched = col_oh.shape
    groups = col_count // lanes
    row_count = row_oh.shape[1]
    grads = values.reshape(slots, levels, 1, touched)
    placed = grads * group_mask[:, None, :, :].astype(jnp.bfloat16)
    lines = jnp.einsum("slaj,sbj->slab", placed, col_oh, preferred_element_type=jnp.bfloat16)
    total = jnp.einsum("sr,slab->lrab", row_oh, lines, preferred_element_type=jnp.float32)
    return total.reshape(levels, row_count, groups * lanes)


def on_device(
    increment_start,
    dual_model_start,
    dual_obs_start,
    model_rhs,
    err_var,
    decays,
    scaling,
    diffusion,
    owners,
    tile_cols,
    jacobian,
    innovation,
    obs_var,
):
    increment = increment_start[0]
    dual_model = dual_model_start[0]
    rhs_field = model_rhs[0]
    err_field = err_var[0]
    decay_field = decays[0]
    owner_list = owners[0]
    cell_index = tile_cols[0]
    observed = innovation[0].astype(jnp.float32)
    obs_error = obs_var[0].astype(jnp.float32)
    obs_dual = dual_obs_start[0].astype(jnp.float32)
    levels, row_count, col_count = increment.shape
    tiles_here, orows, touch_levels = jacobian.shape[1:]
    touched = touch_levels // levels
    owners_count = lax.axis_size("space")
    tm_count = lax.axis_size("tm")
    tm_here = lax.axis_index("tm")
    capacity = max(2, 2 * tiles_here // owners_count)
    slots_all = owners_count * capacity
    groups = col_count // LANES
    diff_coef = diffusion[:, None, None]

    jac_tiles = jacobian[0]

    one_hot = (owner_list[:, None] == jnp.arange(owners_count, dtype=jnp.int32)[None, :]).astype(
        jnp.int32
    )
    earlier_count = jnp.cumsum(one_hot, axis=0) - one_hot
    slot_rank = jnp.sum(earlier_count * one_hot, axis=1)
    position = owner_list * capacity + slot_rank
    slot_oh = (position[:, None] == jnp.arange(slots_all, dtype=jnp.int32)[None, :]).astype(
        jnp.bfloat16
    )
    packed_cells = jnp.zeros((slots_all, touched), jnp.int32).at[position].set(cell_index)
    requests = lax.all_to_all(
        packed_cells.reshape(owners_count, capacity, touched),
        "space",
        split_axis=0,
        concat_axis=0,
        tiled=True,
    ).reshape(slots_all, touched)
    req_rows = requests[:, 0] // col_count
    req_cols = requests % col_count
    row_oh = (req_rows[:, None] == jnp.arange(row_count, dtype=jnp.int32)[None, :])
    col_oh = (
        (req_cols % LANES)[:, None, :] == jnp.arange(LANES, dtype=jnp.int32)[None, :, None]
    ).astype(jnp.bfloat16)
    group_mask = (
        (req_cols // LANES)[:, None, :] == jnp.arange(groups, dtype=jnp.int32)[None, :, None]
    ).astype(jnp.float32)

    scaling_ext = None
    is_first = (tm_here == 0).astype(jnp.float32)
    is_last = (tm_here == tm_count - 1).astype(jnp.float32)

    for repeat in range(ITERS):
        wanted = gather_cols(increment, row_oh.astype(jnp.bfloat16), col_oh, group_mask)
        tile_grad = jnp.einsum(
            "toj,to->tj", jac_tiles, obs_dual.astype(jnp.bfloat16), preferred_element_type=jnp.float32
        ).astype(jnp.bfloat16)
        sent_grad = jnp.einsum(
            "ts,tjl->slj",
            slot_oh,
            tile_grad.reshape(tiles_here, touched, levels),
            preferred_element_type=jnp.float32,
        ).astype(jnp.bfloat16)
        both = jnp.concatenate(
            [
                wanted.reshape(owners_count, capacity * levels, touched),
                sent_grad.reshape(owners_count, capacity * levels, touched),
            ],
            axis=2,
        )
        got = lax.all_to_all(both, "space", split_axis=0, concat_axis=0, tiled=True)
        got_cols = got[:, :, :touched].reshape(slots_all, touch_levels)
        got_grad = got[:, :, touched:].reshape(slots_all, touch_levels)
        own_cols = jnp.einsum(
            "ts,slj->tjl",
            slot_oh,
            got_cols.reshape(slots_all, levels, touched),
            preferred_element_type=jnp.float32,
        ).astype(jnp.bfloat16).reshape(tiles_here, touch_levels)
        obs_image = jnp.einsum(
            "toj,tj->to", jac_tiles, own_cols, preferred_element_type=jnp.float32
        )
        adjoint_field = spread_cols(
            got_grad, row_oh.astype(jnp.bfloat16), col_oh, group_mask, levels, col_count
        )

        if tm_count == 2:
            chosen = jnp.where(tm_here == 0, increment, dual_model)
            if scaling_ext is None:
                both_ext = with_halo(jnp.stack([scaling, chosen]), "space", 2, SUBSTEPS)
                scaling_ext, chosen_ext = both_ext[0], both_ext[1]
            else:
                chosen_ext = with_halo(chosen, "space", 1, SUBSTEPS)
            applied = model_apply(chosen_ext, scaling_ext, diff_coef)
            other = lax.ppermute(applied, "tm", [(0, 1), (1, 0)])
            forward = other * (1.0 - is_first)
            backward = other * (1.0 - is_last)
            r_dual = -(dual_model - backward) - adjoint_field
            decayed = decay_field * r_dual
            if repeat == ITERS - 1:
                own_cols, decayed = lax.optimization_barrier((own_cols, decayed))
                obs_image = jnp.einsum(
                    "toj,tj->to", jac_tiles, own_cols, preferred_element_type=jnp.float32
                )
            upward = r_dual + shifted(decayed, "tm", -1)
        else:
            if scaling_ext is None:
                scaling_ext = with_halo(scaling, "space", 1, SUBSTEPS)
            stacked = jnp.stack([increment, dual_model]).reshape(2 * levels, row_count, col_count)
            applied = model_apply(
                with_halo(stacked, "space", 1, SUBSTEPS),
                jnp.concatenate([scaling_ext, scaling_ext]),
                jnp.concatenate([diff_coef, diff_coef]),
            )
            forward = shifted(applied[:levels], "tm", 1)
            backward = shifted(applied[levels:], "tm", -1)
            r_dual = -(dual_model - backward) - adjoint_field
            upward = r_dual + shifted(decay_field * r_dual, "tm", -1)

        obs_dual = obs_dual + (observed - obs_error * obs_dual - obs_image) / obs_error
        r_model = rhs_field - err_field * dual_model - (increment - forward)
        source = r_model - err_field * upward
        along = source
        along = source + decay_field * shifted(along, "tm", 1)
        dual_model = dual_model + upward
        increment = increment + along
    return (dual_model[None], obs_dual[None], increment[None])


def solution(mesh):
    in_specs = (
        P("tm", None, "space", None),
        P("tm", None, "space", None),
        P("tm", "space", None),
        P("tm", None, "space", None),
        P("tm", None, "space", None),
        P("tm", None, "space", None),
        P(None, "space", None),
        P(),
        P("tm", "space"),
        P("tm", "space", None),
        P("tm", "space", None, None),
        P("tm", "space", None),
        P("tm", "space", None),
    )
    out_specs = (P("tm", None, "space", None), P("tm", "space", None), P("tm", None, "space", None))
    return jax.shard_map(
        on_device, mesh=mesh, in_specs=in_specs, out_specs=out_specs, check_vma=False
    )
```
